128 devices in a mesh: dp: 8 (over z, core), ts: 16 (over y, x).
Axes of the slice: x: 4, y: 4, z: 4, core: 2. Of those that a mesh axis runs over, the one named last changes fastest.
Arguments:
- text_embed: bfloat16 [8, 1024, 4096], P('dp', None, 'ts'), may hold values from -6 to 6
- bridge: bfloat16 [128, 32, 4096], P('dp', None, 'ts'), may hold values from -6 to 6
- crystal_slot: int32 [128], P('dp'), may hold values from 0 to 8159, as said below
- segments: int32 [8, 1024], P('dp'), may hold values from 0 to 15, as said below
- attn_gain: float32 [4096], replicated, may hold values from 0.1 to 1.9
- w_query: bfloat16 [4096, 4096], P(None, 'ts'), as said below
- w_key: bfloat16 [4096, 1024], P(None, 'ts'), may hold values from -0.09375 to 0.09375
- w_value: bfloat16 [4096, 1024], P(None, 'ts'), may hold values from -0.09375 to 0.09375
- w_out: bfloat16 [4096, 4096], P('ts'), may hold values from -0.09375 to 0.09375
- mlp_gain: float32 [4096], replicated, may hold values from 0.1 to 1.9
- w_gate: bfloat16 [4096, 12288], P(None, 'ts'), may hold values from -0.09375 to 0.09375
- w_up: bfloat16 [4096, 12288], P(None, 'ts'), may hold values from -0.09375 to 0.09375
- w_down: bfloat16 [12288, 4096], P('ts'), may hold values from -0.0546875 to 0.0546875
Outputs:
- layer_out: bfloat16 [8, 1024, 4096], P('dp', 'ts')
The draws below stay inside these ranges and needn't reach their ends.
Inputs may be any that keep to these rules, and one draw needn't show every extreme that they name: `segments`: each row starts at 0, never falls and names every document number of 0 to 15; every document holds at least 33 positions. `crystal_slot`: each crystal's 32 rows take the first 32 positions of one document, given as sequence * 1024 + that document's first position; every document takes exactly one crystal, and each sequence takes exactly 2 of the 16 crystals held by each index of dp. `w_query`: entries lie within plus or minus 104 / sqrt(4096).
All inputs are finite; a program needn't handle non-finite values.
Results may differ from the reference program's by a relative error of at most 0.025.
The reference program's roundings to bfloat16 on the way count: a program that leaves them out, or rounds other values in their place, can miss the bound.
Values may be sent and summed in bfloat16 or wider, within the bound.
No kernel may reach another device: no remote copies, remote signals or barrier semaphores. Data moves between devices by JAX's collectives and lax.ppermute only.
A program may use at most 128 MiB of HBM per device.

```python
import jax
import jax.numpy as jnp
from jax import lax

D = 4096
H = 32
KV = 8
HD = 128
FF = 12288
BR = 32
LEN = 1024
SEQS = 8
DOCS = 16
CRYSTALS = 128
N_TS = 16


def one_permutation(one_key):
    return jax.random.permutation(one_key, DOCS)


def layout_tables(key):
    base_key = jax.random.fold_in(key, 7)
    key_lengths, key_docs, key_crystals = jax.random.split(base_key, 3)
    spare_rows = LEN - DOCS * (BR + 1)
    not_last = (jnp.arange(DOCS)[None, :] < DOCS - 1).astype(jnp.int32)
    weights = jax.random.randint(key_lengths, (SEQS, DOCS), 1, 9) * not_last
    extra_rows = weights * spare_rows // jnp.sum(weights, axis=1, keepdims=True)
    extra_rows = extra_rows.at[:, 0].add(spare_rows - jnp.sum(extra_rows, axis=1))
    lengths = BR + 1 + extra_rows
    starts = (jnp.cumsum(lengths, axis=1) - lengths).astype(jnp.int32)
    segment_ids = jnp.sum((starts[:, None, 1:] <= jnp.arange(LEN)[None, :, None]).astype(jnp.int32), axis=2)
    doc_order = jax.vmap(one_permutation)(jax.random.split(key_docs, SEQS))
    crystal_order = jax.vmap(one_permutation)(jax.random.split(key_crystals, SEQS))
    per_group = DOCS // SEQS
    group_ids = jnp.broadcast_to(jnp.arange(SEQS)[:, None], (SEQS, DOCS))
    local_ids = jnp.broadcast_to(jnp.arange(DOCS)[None, :], (SEQS, DOCS))
    seq_ids = local_ids // per_group
    pick_pos = group_ids + SEQS * (local_ids % per_group)
    doc_ids = doc_order[seq_ids, pick_pos]
    slot_values = seq_ids * LEN + starts[seq_ids, doc_ids]
    holder = group_ids * DOCS + crystal_order[group_ids, local_ids]
    crystal_slot = jnp.zeros((CRYSTALS,), jnp.int32).at[holder.reshape(-1)].set(slot_values.reshape(-1).astype(jnp.int32))
    return (segment_ids.astype(jnp.int32), crystal_slot)


def draw_segments(key, part):
    return layout_tables(key)[0]


def draw_crystal_slot(key, part):
    return layout_tables(key)[1]


def draw_w_query(key, part):
    values = jnp.clip(jax.random.normal(key, (D, H * HD), jnp.float32), -6.0, 6.0) / D ** 0.5
    return values.astype(jnp.bfloat16)


def block_levels(rng, shape, pieces, low, largest):
    level = 1.0
    for dim, parts in pieces:
        steps = jax.random.uniform(jax.random.fold_in(jax.random.fold_in(rng, 6), dim), (parts,), jnp.float32, low / len(pieces), largest / len(pieces))
        level = level * jnp.repeat(jnp.exp(steps), shape[dim] // parts).reshape((-1,) + (1,) * (len(shape) - 1 - dim))
    return level


def scatter_about(rng, extent, width, bound, cuts=(), kind=jnp.bfloat16):
    array = jax.random.normal(rng, extent, jnp.float32) * width
    if len(cuts) > 0:
        array = block_levels(rng, extent, cuts, -0.22, 0.18) * array
    return jnp.clip(array, min=-bound, max=bound).astype(kind)


def setup_inputs(seed: int = 0) -> dict:
    seeds = jax.random.split(jax.random.key(seed), 14)
    text_embed = scatter_about(seeds[0], (SEQS, LEN, D), 1.0, 6.0, ((0, 8), (2, 16)))
    bridge = scatter_about(seeds[1], (CRYSTALS, BR, D), 1.0, 6.0, ((0, 8), (2, 16)))
    crystal_slot = draw_crystal_slot(jax.random.fold_in(seeds[13], 71), 0)
    segments = draw_segments(jax.random.fold_in(seeds[13], 71), 0)
    attn_gain = jnp.clip(1.0 + 0.18 * jax.random.normal(seeds[4], (D,), jnp.float32), 0.1, 1.9)
    w_query = draw_w_query(jax.random.fold_in(seeds[13], 71), 0)
    w_key = scatter_about(seeds[6], (D, KV * HD), D ** -0.5, 0.09375, ((1, 16),))
    w_value = scatter_about(seeds[7], (D, KV * HD), D ** -0.5, 0.09375, ((1, 16),))
    w_out = scatter_about(seeds[8], (H * HD, D), (H * HD) ** -0.5, 0.09375, ((0, 16),))
    mlp_gain = jnp.clip(1.0 + 0.18 * jax.random.normal(seeds[9], (D,), jnp.float32), 0.1, 1.9)
    w_gate = scatter_about(seeds[10], (D, FF), D ** -0.5, 0.09375, ((1, 16),))
    w_up = scatter_about(seeds[11], (D, FF), D ** -0.5, 0.09375, ((1, 16),))
    w_down = scatter_about(seeds[12], (FF, D), FF ** -0.5, 0.0546875, ((0, 16),))
    return {"text_embed": text_embed, "bridge": bridge, "crystal_slot": crystal_slot, "segments": segments, "attn_gain": attn_gain, "w_query": w_query, "w_key": w_key, "w_value": w_value, "w_out": w_out, "mlp_gain": mlp_gain, "w_gate": w_gate, "w_up": w_up, "w_down": w_down}


norm_epsilon = 1e-05
rope_base = 500000.0
masked_score = -1e+30

def norm_rows(rows, gain):
    widened = rows.astype(jnp.float32)
    inverse_rms = lax.rsqrt(lax.optimization_barrier(jnp.mean(widened * widened, axis=-1, keepdims=True)) + norm_epsilon)
    return (widened * inverse_rms * gain).astype(jnp.bfloat16)

def rotate_pairs(values, positions, first_pair):
    pair_count = values.shape[-1] // 2
    exponent = 2.0 * (first_pair + jnp.arange(pair_count)).astype(jnp.float32) / HD
    frequency = rope_base ** (-exponent)
    angles = positions.astype(jnp.float32)[:, None] * frequency[None, :]
    cosine = jnp.cos(angles)[:, None, :]
    sine_part = jnp.sin(angles)[:, None, :]
    paired = values.reshape(values.shape[0], values.shape[1], pair_count, 2)
    even_part = paired[..., 0]
    odd_part = paired[..., 1]
    new_even = even_part * cosine - odd_part * sine_part
    new_odd = even_part * sine_part + odd_part * cosine
    return jnp.stack([new_even, new_odd], axis=-1).reshape(values.shape)

def grouped_sum(left, right, group_count):
    group_cols = left.shape[1] // group_count
    total_sum = jnp.zeros((left.shape[0], right.shape[1]), jnp.float32)
    for group_index in range(group_count):
        group_term = jnp.dot(left[:, group_index * group_cols:(group_index + 1) * group_cols], right[group_index * group_cols:(group_index + 1) * group_cols], preferred_element_type=jnp.float32)
        rounded = lax.optimization_barrier(group_term.astype(jnp.bfloat16))
        total_sum = total_sum + rounded.astype(jnp.float32)
    return total_sum

def sequence_layer(packed, segment_ids, attn_gain, w_query, w_key, w_value, w_out, mlp_gain, w_gate, w_up, w_down):
    doc_numbers = jnp.arange(DOCS).astype(jnp.int32)
    starts = lax.optimization_barrier(jnp.sum((segment_ids[None, :] < doc_numbers[:, None]).astype(jnp.int32), axis=1)).astype(jnp.int32)
    positions = (jnp.arange(LEN).astype(jnp.int32) - jnp.take(starts, segment_ids)).astype(jnp.int32)
    normed = norm_rows(packed, attn_gain)
    queries = jnp.dot(normed, w_query, preferred_element_type=jnp.float32).reshape(LEN, H, HD)
    queries = rotate_pairs(queries, positions, 0).astype(jnp.bfloat16)
    keys_all = jnp.dot(normed, w_key, preferred_element_type=jnp.float32).reshape(LEN, KV, HD)
    keys_all = rotate_pairs(keys_all, positions, 0).astype(jnp.bfloat16)
    values_all = jnp.dot(normed, w_value, preferred_element_type=jnp.float32).reshape(LEN, KV, HD).astype(jnp.bfloat16)
    group_size = H // KV
    keys_wide = jnp.repeat(keys_all, group_size, axis=1).astype(jnp.float32)
    values_wide = jnp.repeat(values_all, group_size, axis=1).astype(jnp.float32)
    index_row = jnp.arange(LEN)
    allowed = (segment_ids[:, None] == segment_ids[None, :]) & (index_row[None, :] <= index_row[:, None])
    scores = jnp.einsum('qhd,khd->hqk', queries.astype(jnp.float32), keys_wide) * HD ** (-0.5)
    scores = jnp.where(allowed[None], scores, masked_score)
    row_top = lax.optimization_barrier(jnp.max(scores, axis=-1, keepdims=True))
    weights = jnp.exp(scores - row_top)
    probabilities = (weights / lax.optimization_barrier(jnp.sum(weights, axis=-1, keepdims=True))).astype(jnp.bfloat16)
    attended = jnp.einsum('hqk,khd->qhd', probabilities.astype(jnp.float32), values_wide)
    attended = attended.astype(jnp.bfloat16).reshape(LEN, H * HD)
    attn_sum = grouped_sum(attended, w_out, N_TS)
    after_attn = (packed.astype(jnp.float32) + attn_sum).astype(jnp.bfloat16)
    normed_mlp = norm_rows(after_attn, mlp_gain)
    gate_proj = jnp.dot(normed_mlp, w_gate, preferred_element_type=jnp.float32)
    up_proj = jnp.dot(normed_mlp, w_up, preferred_element_type=jnp.float32)
    hidden = (jax.nn.silu(gate_proj) * up_proj).astype(jnp.bfloat16)
    mlp_sum = grouped_sum(hidden, w_down, N_TS)
    return (after_attn.astype(jnp.float32) + mlp_sum).astype(jnp.bfloat16)

def reference(text_embed, bridge, crystal_slot, segments, attn_gain, w_query, w_key, w_value, w_out, mlp_gain, w_gate, w_up, w_down):
    flat_rows = text_embed.reshape(SEQS * LEN, D)
    target_rows = (crystal_slot[:, None] + jnp.arange(BR).astype(jnp.int32)[None, :]).astype(jnp.int32).reshape(-1)
    flat_rows = flat_rows.at[target_rows].set(bridge.reshape(CRYSTALS * BR, D))
    packed_all = flat_rows.reshape(SEQS, LEN, D)

    def one_sequence(sequence_items):
        return sequence_layer(sequence_items[0], sequence_items[1], attn_gain, w_query, w_key, w_value, w_out, mlp_gain, w_gate, w_up, w_down)
    return lax.map(one_sequence, (packed_all, segments))
```

```python
import jax
import jax.numpy as jnp
from jax import lax
from jax.sharding import PartitionSpec as P

HD = 128
DOC_LEN = 64
ROW_CHUNKS = 2
COL_CHUNKS = 2


norm_epsilon = 1e-05
rope_base = 500000.0
masked_score = -1e30


def partner_2(block, axis, apart):
    count = lax.axis_size(axis)
    route = []
    for low in range(count):
        high = low | 1 << apart
        if high != low and high < count:
            route += [(low, high), (high, low)]
    return lax.ppermute(block, axis, route)


def norm_rows(rows, gain):
    widened = rows.astype(jnp.float32)
    inverse_rms = lax.rsqrt(jnp.mean(widened * widened, axis=-1, keepdims=True) + norm_epsilon)
    return (widened * inverse_rms * gain).astype(jnp.bfloat16)


def rotate_pairs(values, positions, first_pair):
    pair_count = values.shape[-1] // 2
    exponent = 2.0 * (first_pair + jnp.arange(pair_count, dtype=jnp.int32)).astype(jnp.float32) / HD
    frequency = rope_base ** (-exponent)
    angles = positions.astype(jnp.float32)[:, None] * frequency[None, :]
    cosine = jnp.cos(angles)[:, None, :]
    sine_part = jnp.sin(angles)[:, None, :]
    paired = values.reshape(values.shape[0], values.shape[1], pair_count, 2)
    even_part = paired[..., 0]
    odd_part = paired[..., 1]
    new_even = even_part * cosine - odd_part * sine_part
    new_odd = even_part * sine_part + odd_part * cosine
    return jnp.stack([new_even, new_odd], axis=-1).reshape(values.shape)


def attend_block(query_block, query_segments, query_index, keys_full, values_full, segment_ids):
    scores = jnp.einsum(
        "qhd,kd->hqk", query_block, keys_full, preferred_element_type=jnp.float32
    ) * HD ** (-0.5)
    key_index = jnp.arange(keys_full.shape[0], dtype=jnp.int32)
    allowed = (query_segments[:, None] == segment_ids[None, :]) & (
        key_index[None, :] <= query_index[:, None]
    )
    scores = jnp.where(allowed[None], scores, masked_score)
    row_top = jnp.max(scores, axis=-1, keepdims=True)
    weights = jnp.exp(scores - row_top)
    probabilities = (weights / jnp.sum(weights, axis=-1, keepdims=True)).astype(jnp.bfloat16)
    mixed_rows = jnp.einsum(
        "hqk,kd->qhd", probabilities, values_full, preferred_element_type=jnp.float32
    )
    return mixed_rows.astype(jnp.bfloat16).reshape(query_block.shape[0], -1)


def after(ready, value):
    return lax.optimization_barrier((ready, value))[1]


def shards(
    text_embed,
    bridge,
    crystal_slot,
    segments,
    attn_gain,
    w_query,
    w_key,
    w_value,
    w_out,
    mlp_gain,
    w_gate,
    w_up,
    w_down,
):
    seq_len = text_embed.shape[1]
    part_width = text_embed.shape[2]
    doc_count = seq_len // DOC_LEN
    bridge_len = bridge.shape[1]
    tok_rows = seq_len // lax.axis_size("ts")
    group_index = lax.axis_index("dp")
    ts_index = lax.axis_index("ts")
    segment_ids = segments[0]
    doc_numbers = jnp.arange(doc_count, dtype=jnp.int32)
    starts = jnp.sum((segment_ids[None, :] < doc_numbers[:, None]).astype(jnp.int32), axis=1)
    doc_match = segment_ids[:, None] == doc_numbers[None, :]
    positions = jnp.arange(seq_len, dtype=jnp.int32) - jnp.sum(
        jnp.where(doc_match, starts[None, :], 0), axis=1
    )
    flat_bridge = bridge.reshape(bridge.shape[0], bridge_len * part_width)
    slot_high = (crystal_slot // 128).astype(jnp.bfloat16)
    slot_low = (crystal_slot % 128).astype(jnp.bfloat16)
    slot_cols = jnp.zeros((bridge.shape[0], 128), jnp.bfloat16)
    slot_cols = slot_cols.at[:, 0].set(slot_high).at[:, 1].set(slot_low)
    arrived_all = lax.all_gather(
        jnp.concatenate([flat_bridge, slot_cols], axis=1), "dp", axis=0, tiled=True
    )
    arrived = arrived_all[:, : bridge_len * part_width]
    arrived_slots = (
        arrived_all[:, -128].astype(jnp.int32) * 128 + arrived_all[:, -127].astype(jnp.int32)
    )
    wanted = group_index * seq_len + starts
    picking = wanted[:, None] == arrived_slots[None, :]
    by_doc = jnp.dot(
        picking.astype(jnp.bfloat16), arrived, preferred_element_type=jnp.float32
    ).astype(jnp.bfloat16)
    by_doc = by_doc.reshape(doc_count * bridge_len, part_width)
    in_bridge = positions < bridge_len
    row_pick = (segment_ids * bridge_len + positions)[:, None] == jnp.arange(
        doc_count * bridge_len, dtype=jnp.int32
    )[None, :]
    row_pick = row_pick & in_bridge[:, None]
    filled = jnp.dot(
        row_pick.astype(jnp.bfloat16), by_doc, preferred_element_type=jnp.float32
    ).astype(jnp.bfloat16)
    own_part = jnp.where(in_bridge[:, None], filled, text_embed[0])

    chunk_rows = seq_len // ROW_CHUNKS
    heads_here = w_query.shape[1] // HD
    kv_cols = w_key.shape[1]
    upper_half = ts_index % 2 == 1

    packed_chunks = []
    keys_chunks = []
    values_chunks = []
    after_chunks = []
    hidden_chunks = []
    previous = None
    previous_sum = None
    gate = None
    for chunk in range(ROW_CHUNKS):
        rows = slice(chunk * chunk_rows, (chunk + 1) * chunk_rows)
        local_rows = own_part[rows]
        if previous is not None:
            local_rows = after(previous, local_rows)
        packed = lax.all_gather(local_rows, "ts", axis=1, tiled=True)
        previous = packed
        if gate is not None:
            packed = after(gate, packed)
        packed_chunks.append(packed)
        chunk_positions = positions[rows]
        normed = norm_rows(packed, attn_gain)
        queries = jnp.dot(normed, w_query, preferred_element_type=jnp.float32).reshape(
            chunk_rows, heads_here, HD
        )
        queries = rotate_pairs(queries, chunk_positions, 0).astype(jnp.bfloat16)
        key_half = jnp.dot(normed, w_key, preferred_element_type=jnp.float32).reshape(
            chunk_rows, 1, kv_cols
        )
        key_half = rotate_pairs(key_half, chunk_positions, ts_index % 2 * (kv_cols // 2))
        key_half = key_half.astype(jnp.bfloat16).reshape(chunk_rows, kv_cols)
        value_half = jnp.dot(normed, w_value, preferred_element_type=jnp.float32).astype(jnp.bfloat16)
        own_pair = jnp.concatenate([key_half, value_half], axis=1)
        partner = partner_2(own_pair, "ts", 0)
        lower_half = jnp.where(upper_half, partner, own_pair)
        higher = jnp.where(upper_half, own_pair, partner)
        keys_chunks.append(jnp.concatenate([lower_half[:, :kv_cols], higher[:, :kv_cols]], axis=1))
        values_chunks.append(jnp.concatenate([lower_half[:, kv_cols:], higher[:, kv_cols:]], axis=1))
        keys_seen = jnp.concatenate(keys_chunks, axis=0)
        values_seen = jnp.concatenate(values_chunks, axis=0)
        end_row = (chunk + 1) * chunk_rows
        query_index = jnp.arange(chunk * chunk_rows, end_row, dtype=jnp.int32)
        attended = attend_block(
            queries,
            segment_ids[rows],
            query_index,
            keys_seen,
            values_seen,
            segment_ids[:end_row],
        )
        gate = attended
        partial_rows = jnp.dot(attended, w_out, preferred_element_type=jnp.float32).astype(
            jnp.bfloat16
        )
        if previous_sum is not None:
            partial_rows = after(previous_sum, partial_rows)
        attn_sum = lax.psum(partial_rows, "ts")
        previous_sum = attn_sum
        after_attn = (packed.astype(jnp.float32) + attn_sum.astype(jnp.float32)).astype(jnp.bfloat16)
        after_chunks.append(after_attn)
        normed_mlp = norm_rows(after_attn, mlp_gain)
        gate_proj = jnp.dot(normed_mlp, w_gate, preferred_element_type=jnp.float32)
        up_proj = jnp.dot(normed_mlp, w_up, preferred_element_type=jnp.float32)
        hidden_chunks.append((jax.nn.silu(gate_proj) * up_proj).astype(jnp.bfloat16))

    hidden = jnp.concatenate(hidden_chunks, axis=0)
    after_all = jnp.concatenate(after_chunks, axis=0)
    after_mine = lax.dynamic_slice_in_dim(after_all, ts_index * tok_rows, tok_rows, 0)
    out_cols = w_down.shape[1] // COL_CHUNKS
    mlp_parts = []
    previous_part = None
    for col in range(COL_CHUNKS):
        down = jnp.dot(
            hidden, w_down[:, col * out_cols : (col + 1) * out_cols], preferred_element_type=jnp.float32
        ).astype(jnp.bfloat16)
        if previous_part is not None:
            down = after(previous_part, down)
        part = lax.psum_scatter(down, "ts", scatter_dimension=0, tiled=True)
        previous_part = part
        mlp_parts.append(part)
    mlp_mine = jnp.concatenate(mlp_parts, axis=1).astype(jnp.float32)
    layer_rows = (after_mine.astype(jnp.float32) + mlp_mine).astype(jnp.bfloat16)
    return layer_rows.reshape(1, tok_rows, layer_rows.shape[1])


def solution(mesh):
    return jax.shard_map(
        shards,
        mesh=mesh,
        in_specs=(
            P("dp", None, "ts"),
            P("dp", None, "ts"),
            P("dp"),
            P("dp", None),
            P(),
            P(None, "ts"),
            P(None, "ts"),
            P(None, "ts"),
            P("ts", None),
            P(),
            P(None, "ts"),
            P(None, "ts"),
            P("ts", None),
        ),
        out_specs=P("dp", "ts", None),
        check_vma=False,
    )
```

```python
import jax
import jax.numpy as jnp
from jax import lax
from jax.sharding import PartitionSpec as P

HD = 128
DOC_LEN = 64


norm_epsilon = 1e-05
rope_base = 500000.0
masked_score = -1e30


def partner_2(block, axis, apart):
    count = lax.axis_size(axis)
    route = []
    for low in range(count):
        high = low | 1 << apart
        if high != low and high < count:
            route += [(low, high), (high, low)]
    return lax.ppermute(block, axis, route)


def norm_rows(rows, gain):
    widened = rows.astype(jnp.float32)
    inverse_rms = lax.rsqrt(jnp.mean(widened * widened, axis=-1, keepdims=True) + norm_epsilon)
    return (widened * inverse_rms * gain).astype(jnp.bfloat16)


def rotate_pairs(values, positions, first_pair):
    pair_count = values.shape[-1] // 2
    exponent = 2.0 * (first_pair + jnp.arange(pair_count, dtype=jnp.int32)).astype(jnp.float32) / HD
    frequency = rope_base ** (-exponent)
    angles = positions.astype(jnp.float32)[:, None] * frequency[None, :]
    cosine = jnp.cos(angles)[:, None, :]
    sine_part = jnp.sin(angles)[:, None, :]
    paired = values.reshape(values.shape[0], values.shape[1], pair_count, 2)
    even_part = paired[..., 0]
    odd_part = paired[..., 1]
    new_even = even_part * cosine - odd_part * sine_part
    new_odd = even_part * sine_part + odd_part * cosine
    return jnp.stack([new_even, new_odd], axis=-1).reshape(values.shape)


def attend_block(query_block, query_segments, query_index, keys_full, values_full, segment_ids):
    scores = jnp.einsum(
        "qhd,kd->hqk", query_block, keys_full, preferred_element_type=jnp.float32
    ) * HD ** (-0.5)
    key_index = jnp.arange(keys_full.shape[0], dtype=jnp.int32)
    allowed = (query_segments[:, None] == segment_ids[None, :]) & (
        key_index[None, :] <= query_index[:, None]
    )
    scores = jnp.where(allowed[None], scores, masked_score)
    row_top = jnp.max(scores, axis=-1, keepdims=True)
    weights = jnp.exp(scores - row_top)
    probabilities = (weights / jnp.sum(weights, axis=-1, keepdims=True)).astype(jnp.bfloat16)
    mixed_rows = jnp.einsum(
        "hqk,kd->qhd", probabilities, values_full, preferred_element_type=jnp.float32
    )
    return mixed_rows.astype(jnp.bfloat16).reshape(query_block.shape[0], -1)


def shards(
    text_embed,
    bridge,
    crystal_slot,
    segments,
    attn_gain,
    w_query,
    w_key,
    w_value,
    w_out,
    mlp_gain,
    w_gate,
    w_up,
    w_down,
):
    seq_len = text_embed.shape[1]
    part_width = text_embed.shape[2]
    doc_count = seq_len // DOC_LEN
    bridge_len = bridge.shape[1]
    tok_rows = seq_len // lax.axis_size("ts")
    group_index = lax.axis_index("dp")
    ts_index = lax.axis_index("ts")
    segment_ids = segments[0]
    doc_numbers = jnp.arange(doc_count, dtype=jnp.int32)
    starts = jnp.sum((segment_ids[None, :] < doc_numbers[:, None]).astype(jnp.int32), axis=1)
    doc_match = segment_ids[:, None] == doc_numbers[None, :]
    positions = jnp.arange(seq_len, dtype=jnp.int32) - jnp.sum(
        jnp.where(doc_match, starts[None, :], 0), axis=1
    )
    flat_bridge = bridge.reshape(bridge.shape[0], bridge_len * part_width)
    slot_high = (crystal_slot // 128).astype(jnp.bfloat16)
    slot_low = (crystal_slot % 128).astype(jnp.bfloat16)
    slot_cols = jnp.zeros((bridge.shape[0], 128), jnp.bfloat16)
    slot_cols = slot_cols.at[:, 0].set(slot_high).at[:, 1].set(slot_low)
    arrived_all = lax.all_gather(
        jnp.concatenate([flat_bridge, slot_cols], axis=1), "dp", axis=0, tiled=True
    )
    arrived = arrived_all[:, : bridge_len * part_width]
    arrived_slots = (
        arrived_all[:, -128].astype(jnp.int32) * 128 + arrived_all[:, -127].astype(jnp.int32)
    )
    wanted = group_index * seq_len + starts
    picking = wanted[:, None] == arrived_slots[None, :]
    by_doc = jnp.dot(
        picking.astype(jnp.bfloat16), arrived, preferred_element_type=jnp.float32
    ).astype(jnp.bfloat16)
    by_doc = by_doc.reshape(doc_count * bridge_len, part_width)
    in_bridge = positions < bridge_len
    row_pick = (segment_ids * bridge_len + positions)[:, None] == jnp.arange(
        doc_count * bridge_len, dtype=jnp.int32
    )[None, :]
    row_pick = row_pick & in_bridge[:, None]
    filled = jnp.dot(
        row_pick.astype(jnp.bfloat16), by_doc, preferred_element_type=jnp.float32
    ).astype(jnp.bfloat16)
    own_part = jnp.where(in_bridge[:, None], filled, text_embed[0])
    packed = lax.all_gather(own_part, "ts", axis=1, tiled=True)
    normed = norm_rows(packed, attn_gain)
    heads_here = w_query.shape[1] // HD
    queries = jnp.dot(normed, w_query, preferred_element_type=jnp.float32).reshape(
        seq_len, heads_here, HD
    )
    queries = rotate_pairs(queries, positions, 0).astype(jnp.bfloat16)
    kv_cols = w_key.shape[1]
    upper_half = ts_index % 2 == 1
    key_half = jnp.dot(normed, w_key, preferred_element_type=jnp.float32).reshape(
        seq_len, 1, kv_cols
    )
    key_half = rotate_pairs(key_half, positions, ts_index % 2 * (kv_cols // 2))
    key_half = key_half.astype(jnp.bfloat16).reshape(seq_len, kv_cols)
    value_half = jnp.dot(normed, w_value, preferred_element_type=jnp.float32).astype(jnp.bfloat16)
    own_pair = jnp.concatenate([key_half, value_half], axis=1)
    partner = partner_2(own_pair, "ts", 0)
    lower_half = jnp.where(upper_half, partner, own_pair)
    higher = jnp.where(upper_half, own_pair, partner)
    keys_full = jnp.concatenate([lower_half[:, :kv_cols], higher[:, :kv_cols]], axis=1)
    values_full = jnp.concatenate([lower_half[:, kv_cols:], higher[:, kv_cols:]], axis=1)
    block_rows = min(512, seq_len)
    outputs = []
    for block_index in range(seq_len // block_rows):
        first_row = block_index * block_rows
        query_index = jnp.arange(first_row, first_row + block_rows, dtype=jnp.int32)
        outputs.append(
            attend_block(
                queries[first_row : first_row + block_rows],
                segment_ids[first_row : first_row + block_rows],
                query_index,
                keys_full,
                values_full,
                segment_ids,
            )
        )
    attended = jnp.concatenate(outputs, axis=0)
    mine_offset = ts_index * tok_rows
    partial_rows = jnp.dot(attended, w_out, preferred_element_type=jnp.float32)
    attn_sum = lax.psum(partial_rows.astype(jnp.bfloat16), "ts").astype(jnp.float32)
    after_all = (packed.astype(jnp.float32) + attn_sum).astype(jnp.bfloat16)
    after_mine = lax.dynamic_slice_in_dim(after_all, mine_offset, tok_rows, 0)
    normed_mlp = norm_rows(after_all, mlp_gain)
    gate_proj = jnp.dot(normed_mlp, w_gate, preferred_element_type=jnp.float32)
    up_proj = jnp.dot(normed_mlp, w_up, preferred_element_type=jnp.float32)
    hidden = (jax.nn.silu(gate_proj) * up_proj).astype(jnp.bfloat16)
    mlp_mine = lax.psum_scatter(
        jnp.dot(hidden, w_down, preferred_element_type=jnp.float32).astype(jnp.bfloat16),
        "ts",
        scatter_dimension=0,
        tiled=True,
    ).astype(jnp.float32)
    layer_rows = (after_mine.astype(jnp.float32) + mlp_mine).astype(jnp.bfloat16)
    return layer_rows.reshape(1, tok_rows, layer_rows.shape[1])


def solution(mesh):
    return jax.shard_map(
        shards,
        mesh=mesh,
        in_specs=(
            P("dp", None, "ts"),
            P("dp", None, "ts"),
            P("dp"),
            P("dp", None),
            P(),
            P(None, "ts"),
            P(None, "ts"),
            P(None, "ts"),
            P("ts", None),
            P(),
            P(None, "ts"),
            P(None, "ts"),
            P("ts", None),
        ),
        out_specs=P("dp", "ts", None),
        check_vma=False,
    )
```

```python
import jax
import jax.numpy as jnp
from jax import lax
from jax.sharding import PartitionSpec as P

HD = 128
DOC_LEN = 64


norm_epsilon = 1e-05
rope_base = 500000.0
masked_score = -1e30


def partner_2(block, axis, apart):
    count = lax.axis_size(axis)
    route = []
    for low in range(count):
        high = low | 1 << apart
        if high != low and high < count:
            route += [(low, high), (high, low)]
    return lax.ppermute(block, axis, route)


def norm_rows(rows, gain):
    widened = rows.astype(jnp.float32)
    inverse_rms = lax.rsqrt(jnp.mean(widened * widened, axis=-1, keepdims=True) + norm_epsilon)
    return (widened * inverse_rms * gain).astype(jnp.bfloat16)


def rotate_pairs(values, positions, first_pair):
    pair_count = values.shape[-1] // 2
    exponent = 2.0 * (first_pair + jnp.arange(pair_count, dtype=jnp.int32)).astype(jnp.float32) / HD
    frequency = rope_base ** (-exponent)
    angles = positions.astype(jnp.float32)[:, None] * frequency[None, :]
    cosine = jnp.cos(angles)[:, None, :]
    sine_part = jnp.sin(angles)[:, None, :]
    paired = values.reshape(values.shape[0], values.shape[1], pair_count, 2)
    even_part = paired[..., 0]
    odd_part = paired[..., 1]
    new_even = even_part * cosine - odd_part * sine_part
    new_odd = even_part * sine_part + odd_part * cosine
    return jnp.stack([new_even, new_odd], axis=-1).reshape(values.shape)


def attend_block(query_block, query_segments, query_index, keys_full, values_full, segment_ids):
    scores = jnp.einsum(
        "qhd,kd->hqk", query_block, keys_full, preferred_element_type=jnp.float32
    ) * HD ** (-0.5)
    key_index = jnp.arange(keys_full.shape[0], dtype=jnp.int32)
    allowed = (query_segments[:, None] == segment_ids[None, :]) & (
        key_index[None, :] <= query_index[:, None]
    )
    scores = jnp.where(allowed[None], scores, masked_score)
    row_top = jnp.max(scores, axis=-1, keepdims=True)
    weights = jnp.exp(scores - row_top)
    probabilities = (weights / jnp.sum(weights, axis=-1, keepdims=True)).astype(jnp.bfloat16)
    mixed_rows = jnp.einsum(
        "hqk,kd->qhd", probabilities, values_full, preferred_element_type=jnp.float32
    )
    return mixed_rows.astype(jnp.bfloat16).reshape(query_block.shape[0], -1)


def shards(
    text_embed,
    bridge,
    crystal_slot,
    segments,
    attn_gain,
    w_query,
    w_key,
    w_value,
    w_out,
    mlp_gain,
    w_gate,
    w_up,
    w_down,
):
    seq_len = text_embed.shape[1]
    part_width = text_embed.shape[2]
    doc_count = seq_len // DOC_LEN
    bridge_len = bridge.shape[1]
    tok_rows = seq_len // lax.axis_size("ts")
    group_index = lax.axis_index("dp")
    ts_index = lax.axis_index("ts")
    segment_ids = segments[0]
    doc_numbers = jnp.arange(doc_count, dtype=jnp.int32)
    starts = jnp.sum((segment_ids[None, :] < doc_numbers[:, None]).astype(jnp.int32), axis=1)
    doc_match = segment_ids[:, None] == doc_numbers[None, :]
    positions = jnp.arange(seq_len, dtype=jnp.int32) - jnp.sum(
        jnp.where(doc_match, starts[None, :], 0), axis=1
    )
    flat_bridge = bridge.reshape(bridge.shape[0], bridge_len * part_width)
    slot_high = (crystal_slot // 128).astype(jnp.bfloat16)
    slot_low = (crystal_slot % 128).astype(jnp.bfloat16)
    slot_cols = jnp.zeros((bridge.shape[0], 128), jnp.bfloat16)
    slot_cols = slot_cols.at[:, 0].set(slot_high).at[:, 1].set(slot_low)
    payload = jnp.concatenate([flat_bridge, slot_cols], axis=1)
    crystal_count = bridge.shape[0]
    destination = crystal_slot // seq_len
    crystal_numbers = jnp.arange(crystal_count, dtype=jnp.int32)
    same_destination = destination[:, None] == destination[None, :]
    rank = jnp.sum(
        (same_destination & (crystal_numbers[None, :] < crystal_numbers[:, None])).astype(jnp.int32),
        axis=1,
    )
    per_destination = crystal_count // lax.axis_size("dp")
    send_row = destination * per_destination + rank
    sending = crystal_numbers[:, None] == send_row[None, :]
    outgoing = jnp.dot(
        sending.astype(jnp.bfloat16), payload, preferred_element_type=jnp.float32
    ).astype(jnp.bfloat16)
    arrived_all = lax.all_to_all(outgoing, "dp", 0, 0, tiled=True)
    arrived = arrived_all[:, : bridge_len * part_width]
    arrived_slots = (
        arrived_all[:, -128].astype(jnp.int32) * 128 + arrived_all[:, -127].astype(jnp.int32)
    )
    wanted = group_index * seq_len + starts
    picking = wanted[:, None] == arrived_slots[None, :]
    by_doc = jnp.dot(
        picking.astype(jnp.bfloat16), arrived, preferred_element_type=jnp.float32
    ).astype(jnp.bfloat16)
    by_doc = by_doc.reshape(doc_count * bridge_len, part_width)
    in_bridge = positions < bridge_len
    row_pick = (segment_ids * bridge_len + positions)[:, None] == jnp.arange(
        doc_count * bridge_len, dtype=jnp.int32
    )[None, :]
    row_pick = row_pick & in_bridge[:, None]
    filled = jnp.dot(
        row_pick.astype(jnp.bfloat16), by_doc, preferred_element_type=jnp.float32
    ).astype(jnp.bfloat16)
    own_part = jnp.where(in_bridge[:, None], filled, text_embed[0])
    packed = lax.all_gather(own_part, "ts", axis=1, tiled=True)
    normed = norm_rows(packed, attn_gain)
    heads_here = w_query.shape[1] // HD
    queries = jnp.dot(normed, w_query, preferred_element_type=jnp.float32).reshape(
        seq_len, heads_here, HD
    )
    queries = rotate_pairs(queries, positions, 0).astype(jnp.bfloat16)
    kv_cols = w_key.shape[1]
    upper_half = ts_index % 2 == 1
    key_half = jnp.dot(normed, w_key, preferred_element_type=jnp.float32).reshape(
        seq_len, 1, kv_cols
    )
    key_half = rotate_pairs(key_half, positions, ts_index % 2 * (kv_cols // 2))
    key_half = key_half.astype(jnp.bfloat16).reshape(seq_len, kv_cols)
    value_half = jnp.dot(normed, w_value, preferred_element_type=jnp.float32).astype(jnp.bfloat16)
    own_pair = jnp.concatenate([key_half, value_half], axis=1)
    partner = partner_2(own_pair, "ts", 0)
    lower_half = jnp.where(upper_half, partner, own_pair)
    higher = jnp.where(upper_half, own_pair, partner)
    keys_full = jnp.concatenate([lower_half[:, :kv_cols], higher[:, :kv_cols]], axis=1)
    values_full = jnp.concatenate([lower_half[:, kv_cols:], higher[:, kv_cols:]], axis=1)
    block_rows = min(512, seq_len)
    outputs = []
    for block_index in range(seq_len // block_rows):
        first_row = block_index * block_rows
        query_index = jnp.arange(first_row, first_row + block_rows, dtype=jnp.int32)
        outputs.append(
            attend_block(
                queries[first_row : first_row + block_rows],
                segment_ids[first_row : first_row + block_rows],
                query_index,
                keys_full,
                values_full,
                segment_ids,
            )
        )
    attended = jnp.concatenate(outputs, axis=0)
    mine_offset = ts_index * tok_rows
    partial_rows = jnp.dot(attended, w_out, preferred_element_type=jnp.float32)
    attn_sum = lax.psum(partial_rows.astype(jnp.bfloat16), "ts").astype(jnp.float32)
    after_all = (packed.astype(jnp.float32) + attn_sum).astype(jnp.bfloat16)
    after_mine = lax.dynamic_slice_in_dim(after_all, mine_offset, tok_rows, 0)
    normed_mlp = norm_rows(after_all, mlp_gain)
    gate_proj = jnp.dot(normed_mlp, w_gate, preferred_element_type=jnp.float32)
    up_proj = jnp.dot(normed_mlp, w_up, preferred_element_type=jnp.float32)
    hidden = (jax.nn.silu(gate_proj) * up_proj).astype(jnp.bfloat16)
    mlp_mine = lax.psum_scatter(
        jnp.dot(hidden, w_down, preferred_element_type=jnp.float32).astype(jnp.bfloat16),
        "ts",
        scatter_dimension=0,
        tiled=True,
    ).astype(jnp.float32)
    layer_rows = (after_mine.astype(jnp.float32) + mlp_mine).astype(jnp.bfloat16)
    return layer_rows.reshape(1, tok_rows, layer_rows.shape[1])


def solution(mesh):
    return jax.shard_map(
        shards,
        mesh=mesh,
        in_specs=(
            P("dp", None, "ts"),
            P("dp", None, "ts"),
            P("dp"),
            P("dp", None),
            P(),
            P(None, "ts"),
            P(None, "ts"),
            P(None, "ts"),
            P("ts", None),
            P(),
            P(None, "ts"),
            P(None, "ts"),
            P("ts", None),
        ),
        out_specs=P("dp", "ts", None),
        check_vma=False,
    )
```

```python
import jax
import jax.numpy as jnp
from jax import lax
from jax.sharding import PartitionSpec as P

HD = 128
DOC_LEN = 64


norm_epsilon = 1e-05
rope_base = 500000.0
masked_score = -1e30


def partner_2(block, axis, apart):
    count = lax.axis_size(axis)
    route = []
    for low in range(count):
        high = low | 1 << apart
        if high != low and high < count:
            route += [(low, high), (high, low)]
    return lax.ppermute(block, axis, route)


def norm_rows(rows, gain):
    widened = rows.astype(jnp.float32)
    inverse_rms = lax.rsqrt(jnp.mean(widened * widened, axis=-1, keepdims=True) + norm_epsilon)
    return (widened * inverse_rms * gain).astype(jnp.bfloat16)


def rotate_pairs(values, positions, first_pair):
    pair_count = values.shape[-1] // 2
    exponent = 2.0 * (first_pair + jnp.arange(pair_count, dtype=jnp.int32)).astype(jnp.float32) / HD
    frequency = rope_base ** (-exponent)
    angles = positions.astype(jnp.float32)[:, None] * frequency[None, :]
    cosine = jnp.cos(angles)[:, None, :]
    sine_part = jnp.sin(angles)[:, None, :]
    paired = values.reshape(values.shape[0], values.shape[1], pair_count, 2)
    even_part = paired[..., 0]
    odd_part = paired[..., 1]
    new_even = even_part * cosine - odd_part * sine_part
    new_odd = even_part * sine_part + odd_part * cosine
    return jnp.stack([new_even, new_odd], axis=-1).reshape(values.shape)


def attend_block(query_block, query_segments, query_index, keys_full, values_full, segment_ids):
    scores = jnp.einsum(
        "qhd,kd->hqk", query_block, keys_full, preferred_element_type=jnp.float32
    ) * HD ** (-0.5)
    key_index = jnp.arange(keys_full.shape[0], dtype=jnp.int32)
    allowed = (query_segments[:, None] == segment_ids[None, :]) & (
        key_index[None, :] <= query_index[:, None]
    )
    scores = jnp.where(allowed[None], scores, masked_score)
    row_top = jnp.max(scores, axis=-1, keepdims=True)
    weights = jnp.exp(scores - row_top)
    probabilities = (weights / jnp.sum(weights, axis=-1, keepdims=True)).astype(jnp.bfloat16)
    mixed_rows = jnp.einsum(
        "hqk,kd->qhd", probabilities, values_full, preferred_element_type=jnp.float32
    )
    return mixed_rows.astype(jnp.bfloat16).reshape(query_block.shape[0], -1)


def shards(
    text_embed,
    bridge,
    crystal_slot,
    segments,
    attn_gain,
    w_query,
    w_key,
    w_value,
    w_out,
    mlp_gain,
    w_gate,
    w_up,
    w_down,
):
    seq_len = text_embed.shape[1]
    part_width = text_embed.shape[2]
    doc_count = seq_len // DOC_LEN
    bridge_len = bridge.shape[1]
    tok_rows = seq_len // lax.axis_size("ts")
    group_index = lax.axis_index("dp")
    ts_index = lax.axis_index("ts")
    segment_ids = segments[0]
    doc_numbers = jnp.arange(doc_count, dtype=jnp.int32)
    starts = jnp.sum((segment_ids[None, :] < doc_numbers[:, None]).astype(jnp.int32), axis=1)
    doc_match = segment_ids[:, None] == doc_numbers[None, :]
    positions = jnp.arange(seq_len, dtype=jnp.int32) - jnp.sum(
        jnp.where(doc_match, starts[None, :], 0), axis=1
    )
    flat_bridge = bridge.reshape(bridge.shape[0], bridge_len * part_width)
    slot_high = (crystal_slot // 128).astype(jnp.bfloat16)
    slot_low = (crystal_slot % 128).astype(jnp.bfloat16)
    slot_cols = jnp.zeros((bridge.shape[0], 128), jnp.bfloat16)
    slot_cols = slot_cols.at[:, 0].set(slot_high).at[:, 1].set(slot_low)
    payload = jnp.concatenate([flat_bridge, slot_cols], axis=1)
    crystal_count = bridge.shape[0]
    destination = crystal_slot // seq_len
    crystal_numbers = jnp.arange(crystal_count, dtype=jnp.int32)
    same_destination = destination[:, None] == destination[None, :]
    rank = jnp.sum(
        (same_destination & (crystal_numbers[None, :] < crystal_numbers[:, None])).astype(jnp.int32),
        axis=1,
    )
    per_destination = crystal_count // lax.axis_size("dp")
    send_row = destination * per_destination + rank
    sending = crystal_numbers[:, None] == send_row[None, :]
    outgoing = jnp.dot(
        sending.astype(jnp.bfloat16), payload, preferred_element_type=jnp.float32
    ).astype(jnp.bfloat16)
    arrived_all = lax.all_to_all(outgoing, "dp", 0, 0, tiled=True)
    arrived = arrived_all[:, : bridge_len * part_width]
    arrived_slots = (
        arrived_all[:, -128].astype(jnp.int32) * 128 + arrived_all[:, -127].astype(jnp.int32)
    )
    wanted = group_index * seq_len + starts
    picking = wanted[:, None] == arrived_slots[None, :]
    by_doc = jnp.dot(
        picking.astype(jnp.bfloat16), arrived, preferred_element_type=jnp.float32
    ).astype(jnp.bfloat16)
    by_doc = by_doc.reshape(doc_count * bridge_len, part_width)
    in_bridge = positions < bridge_len
    row_pick = (segment_ids * bridge_len + positions)[:, None] == jnp.arange(
        doc_count * bridge_len, dtype=jnp.int32
    )[None, :]
    row_pick = row_pick & in_bridge[:, None]
    filled = jnp.dot(
        row_pick.astype(jnp.bfloat16), by_doc, preferred_element_type=jnp.float32
    ).astype(jnp.bfloat16)
    own_part = jnp.where(in_bridge[:, None], filled, text_embed[0])
    packed = lax.all_gather(own_part, "ts", axis=1, tiled=True)
    positions = lax.optimization_barrier((own_part, positions))[1]
    normed = norm_rows(packed, attn_gain)
    heads_here = w_query.shape[1] // HD
    queries = jnp.dot(normed, w_query, preferred_element_type=jnp.float32).reshape(
        seq_len, heads_here, HD
    )
    queries = rotate_pairs(queries, positions, 0).astype(jnp.bfloat16)
    kv_cols = w_key.shape[1]
    upper_half = ts_index % 2 == 1
    key_half = jnp.dot(normed, w_key, preferred_element_type=jnp.float32).reshape(
        seq_len, 1, kv_cols
    )
    key_half = rotate_pairs(key_half, positions, ts_index % 2 * (kv_cols // 2))
    key_half = key_half.astype(jnp.bfloat16).reshape(seq_len, kv_cols)
    value_half = jnp.dot(normed, w_value, preferred_element_type=jnp.float32).astype(jnp.bfloat16)
    own_pair = jnp.concatenate([key_half, value_half], axis=1)
    partner = partner_2(own_pair, "ts", 0)
    lower_half = jnp.where(upper_half, partner, own_pair)
    higher = jnp.where(upper_half, own_pair, partner)
    keys_full = jnp.concatenate([lower_half[:, :kv_cols], higher[:, :kv_cols]], axis=1)
    values_full = jnp.concatenate([lower_half[:, kv_cols:], higher[:, kv_cols:]], axis=1)
    block_rows = min(512, seq_len)
    outputs = []
    for block_index in range(seq_len // block_rows):
        first_row = block_index * block_rows
        end_row = first_row + block_rows
        query_index = jnp.arange(first_row, end_row, dtype=jnp.int32)
        outputs.append(
            attend_block(
                queries[first_row:end_row],
                segment_ids[first_row:end_row],
                query_index,
                keys_full[:end_row],
                values_full[:end_row],
                segment_ids[:end_row],
            )
        )
    attended = jnp.concatenate(outputs, axis=0)
    mine_offset = ts_index * tok_rows
    partial_rows = jnp.dot(attended, w_out, preferred_element_type=jnp.float32)
    attn_sum = lax.psum(partial_rows.astype(jnp.bfloat16), "ts").astype(jnp.float32)
    after_all = (packed.astype(jnp.float32) + attn_sum).astype(jnp.bfloat16)
    after_mine = lax.dynamic_slice_in_dim(after_all, mine_offset, tok_rows, 0)
    normed_mlp = norm_rows(after_all, mlp_gain)
    gate_proj = jnp.dot(normed_mlp, w_gate, preferred_element_type=jnp.float32)
    up_proj = jnp.dot(normed_mlp, w_up, preferred_element_type=jnp.float32)
    hidden = (jax.nn.silu(gate_proj) * up_proj).astype(jnp.bfloat16)
    mlp_mine = lax.psum_scatter(
        jnp.dot(hidden, w_down, preferred_element_type=jnp.float32).astype(jnp.bfloat16),
        "ts",
        scatter_dimension=0,
        tiled=True,
    ).astype(jnp.float32)
    layer_rows = (after_mine.astype(jnp.float32) + mlp_mine).astype(jnp.bfloat16)
    return layer_rows.reshape(1, tok_rows, layer_rows.shape[1])


def solution(mesh):
    return jax.shard_map(
        shards,
        mesh=mesh,
        in_specs=(
            P("dp", None, "ts"),
            P("dp", None, "ts"),
            P("dp"),
            P("dp", None),
            P(),
            P(None, "ts"),
            P(None, "ts"),
            P(None, "ts"),
            P("ts", None),
            P(),
            P(None, "ts"),
            P(None, "ts"),
            P("ts", None),
        ),
        out_specs=P("dp", "ts", None),
        check_vma=False,
    )
```

```python
import jax
import jax.numpy as jnp
from jax import lax
from jax.sharding import PartitionSpec as P

HD = 128
DOC_LEN = 64


norm_epsilon = 1e-05
rope_base = 500000.0
masked_score = -1e30


def partner_2(block, axis, apart):
    count = lax.axis_size(axis)
    route = []
    for low in range(count):
        high = low | 1 << apart
        if high != low and high < count:
            route += [(low, high), (high, low)]
    return lax.ppermute(block, axis, route)


def norm_rows(rows, gain):
    widened = rows.astype(jnp.float32)
    inverse_rms = lax.rsqrt(jnp.mean(widened * widened, axis=-1, keepdims=True) + norm_epsilon)
    return (widened * inverse_rms * gain).astype(jnp.bfloat16)


def rotate_pairs(values, positions, first_pair):
    pair_count = values.shape[-1] // 2
    exponent = 2.0 * (first_pair + jnp.arange(pair_count, dtype=jnp.int32)).astype(jnp.float32) / HD
    frequency = rope_base ** (-exponent)
    angles = positions.astype(jnp.float32)[:, None] * frequency[None, :]
    cosine = jnp.cos(angles)[:, None, :]
    sine_part = jnp.sin(angles)[:, None, :]
    paired = values.reshape(values.shape[0], values.shape[1], pair_count, 2)
    even_part = paired[..., 0]
    odd_part = paired[..., 1]
    new_even = even_part * cosine - odd_part * sine_part
    new_odd = even_part * sine_part + odd_part * cosine
    return jnp.stack([new_even, new_odd], axis=-1).reshape(values.shape)


def attend_block(query_block, query_segments, query_index, keys_full, values_full, segment_ids):
    scores = jnp.einsum(
        "qhd,kd->hqk", query_block, keys_full, preferred_element_type=jnp.float32
    ) * HD ** (-0.5)
    key_index = jnp.arange(keys_full.shape[0], dtype=jnp.int32)
    allowed = (query_segments[:, None] == segment_ids[None, :]) & (
        key_index[None, :] <= query_index[:, None]
    )
    scores = jnp.where(allowed[None], scores, masked_score)
    row_top = jnp.max(scores, axis=-1, keepdims=True)
    weights = jnp.exp(scores - row_top)
    probabilities = (weights / jnp.sum(weights, axis=-1, keepdims=True)).astype(jnp.bfloat16)
    mixed_rows = jnp.einsum(
        "hqk,kd->qhd", probabilities, values_full, preferred_element_type=jnp.float32
    )
    return mixed_rows.astype(jnp.bfloat16).reshape(query_block.shape[0], -1)


def shards(
    text_embed,
    bridge,
    crystal_slot,
    segments,
    attn_gain,
    w_query,
    w_key,
    w_value,
    w_out,
    mlp_gain,
    w_gate,
    w_up,
    w_down,
):
    seq_len = text_embed.shape[1]
    part_width = text_embed.shape[2]
    doc_count = seq_len // DOC_LEN
    bridge_len = bridge.shape[1]
    tok_rows = seq_len // lax.axis_size("ts")
    group_index = lax.axis_index("dp")
    ts_index = lax.axis_index("ts")
    segment_ids = segments[0]
    doc_numbers = jnp.arange(doc_count, dtype=jnp.int32)
    starts = jnp.sum((segment_ids[None, :] < doc_numbers[:, None]).astype(jnp.int32), axis=1)
    doc_match = segment_ids[:, None] == doc_numbers[None, :]
    positions = jnp.arange(seq_len, dtype=jnp.int32) - jnp.sum(
        jnp.where(doc_match, starts[None, :], 0), axis=1
    )
    flat_bridge = bridge.reshape(bridge.shape[0], bridge_len * part_width)
    slot_high = (crystal_slot // 128).astype(jnp.bfloat16)
    slot_low = (crystal_slot % 128).astype(jnp.bfloat16)
    slot_cols = jnp.zeros((bridge.shape[0], 128), jnp.bfloat16)
    slot_cols = slot_cols.at[:, 0].set(slot_high).at[:, 1].set(slot_low)
    payload = jnp.concatenate([flat_bridge, slot_cols], axis=1)
    crystal_count = bridge.shape[0]
    destination = crystal_slot // seq_len
    crystal_numbers = jnp.arange(crystal_count, dtype=jnp.int32)
    same_destination = destination[:, None] == destination[None, :]
    rank = jnp.sum(
        (same_destination & (crystal_numbers[None, :] < crystal_numbers[:, None])).astype(jnp.int32),
        axis=1,
    )
    per_destination = crystal_count // lax.axis_size("dp")
    send_row = destination * per_destination + rank
    sending = crystal_numbers[:, None] == send_row[None, :]
    outgoing = jnp.dot(
        sending.astype(jnp.bfloat16), payload, preferred_element_type=jnp.float32
    ).astype(jnp.bfloat16)
    arrived_all = lax.all_to_all(outgoing, "dp", 0, 0, tiled=True)
    arrived = arrived_all[:, : bridge_len * part_width]
    arrived_slots = (
        arrived_all[:, -128].astype(jnp.int32) * 128 + arrived_all[:, -127].astype(jnp.int32)
    )
    wanted = group_index * seq_len + starts
    picking = wanted[:, None] == arrived_slots[None, :]
    by_doc = jnp.dot(
        picking.astype(jnp.bfloat16), arrived, preferred_element_type=jnp.float32
    ).astype(jnp.bfloat16)
    by_doc = by_doc.reshape(doc_count * bridge_len, part_width)
    in_bridge = positions < bridge_len
    row_pick = (segment_ids * bridge_len + positions)[:, None] == jnp.arange(
        doc_count * bridge_len, dtype=jnp.int32
    )[None, :]
    row_pick = row_pick & in_bridge[:, None]
    filled = jnp.dot(
        row_pick.astype(jnp.bfloat16), by_doc, preferred_element_type=jnp.float32
    ).astype(jnp.bfloat16)
    own_part = jnp.where(in_bridge[:, None], filled, text_embed[0])
    ts_count = lax.axis_size("ts")
    stacked = lax.all_gather(own_part, "ts", axis=0, tiled=False)
    positions = lax.optimization_barrier((own_part, positions))[1]
    packed = lax.optimization_barrier(
        stacked.transpose(1, 0, 2).reshape(seq_len, ts_count * part_width)
    )
    widened = stacked.astype(jnp.float32)
    square_sum = jnp.sum(jnp.sum(widened * widened, axis=2), axis=0)
    inverse_rms = lax.rsqrt(square_sum / (ts_count * part_width) + norm_epsilon)
    normed = (
        widened * inverse_rms[None, :, None] * attn_gain.reshape(ts_count, 1, part_width)
    ).astype(jnp.bfloat16)

    def project(weight):
        return jnp.einsum(
            "srk,skn->rn",
            normed,
            weight.reshape(ts_count, part_width, weight.shape[1]),
            preferred_element_type=jnp.float32,
        )

    heads_here = w_query.shape[1] // HD
    queries = project(w_query).reshape(seq_len, heads_here, HD)
    queries = rotate_pairs(queries, positions, 0).astype(jnp.bfloat16)
    kv_cols = w_key.shape[1]
    upper_half = ts_index % 2 == 1
    key_half = project(w_key).reshape(
        seq_len, 1, kv_cols
    )
    key_half = rotate_pairs(key_half, positions, ts_index % 2 * (kv_cols // 2))
    key_half = key_half.astype(jnp.bfloat16).reshape(seq_len, kv_cols)
    value_half = project(w_value).astype(jnp.bfloat16)
    own_pair = jnp.concatenate([key_half, value_half], axis=1)
    partner = partner_2(own_pair, "ts", 0)
    lower_half = jnp.where(upper_half, partner, own_pair)
    higher = jnp.where(upper_half, own_pair, partner)
    keys_full = jnp.concatenate([lower_half[:, :kv_cols], higher[:, :kv_cols]], axis=1)
    values_full = jnp.concatenate([lower_half[:, kv_cols:], higher[:, kv_cols:]], axis=1)
    block_rows = min(512, seq_len)
    outputs = []
    for block_index in range(seq_len // block_rows):
        first_row = block_index * block_rows
        end_row = first_row + block_rows
        query_index = jnp.arange(first_row, end_row, dtype=jnp.int32)
        outputs.append(
            attend_block(
                queries[first_row:end_row],
                segment_ids[first_row:end_row],
                query_index,
                keys_full[:end_row],
                values_full[:end_row],
                segment_ids[:end_row],
            )
        )
    attended = jnp.concatenate(outputs, axis=0)
    mine_offset = ts_index * tok_rows
    partial_rows = jnp.dot(attended, w_out, preferred_element_type=jnp.float32)
    attn_sum = lax.psum(partial_rows.astype(jnp.bfloat16), "ts").astype(jnp.float32)
    after_all = (packed.astype(jnp.float32) + attn_sum).astype(jnp.bfloat16)
    after_mine = lax.dynamic_slice_in_dim(after_all, mine_offset, tok_rows, 0)
    normed_mlp = norm_rows(after_all, mlp_gain)
    gate_proj = jnp.dot(normed_mlp, w_gate, preferred_element_type=jnp.float32)
    up_proj = jnp.dot(normed_mlp, w_up, preferred_element_type=jnp.float32)
    hidden = (jax.nn.silu(gate_proj) * up_proj).astype(jnp.bfloat16)
    mlp_mine = lax.psum_scatter(
        jnp.dot(hidden, w_down, preferred_element_type=jnp.float32).astype(jnp.bfloat16),
        "ts",
        scatter_dimension=0,
        tiled=True,
    ).astype(jnp.float32)
    layer_rows = (after_mine.astype(jnp.float32) + mlp_mine).astype(jnp.bfloat16)
    return layer_rows.reshape(1, tok_rows, layer_rows.shape[1])


def solution(mesh):
    return jax.shard_map(
        shards,
        mesh=mesh,
        in_specs=(
            P("dp", None, "ts"),
            P("dp", None, "ts"),
            P("dp"),
            P("dp", None),
            P(),
            P(None, "ts"),
            P(None, "ts"),
            P(None, "ts"),
            P("ts", None),
            P(),
            P(None, "ts"),
            P(None, "ts"),
            P("ts", None),
        ),
        out_specs=P("dp", "ts", None),
        check_vma=False,
    )
```

```python
import jax
import jax.numpy as jnp
from jax import lax
from jax.sharding import PartitionSpec as P

HD = 128
DOC_LEN = 64


norm_epsilon = 1e-05
rope_base = 500000.0
masked_score = -1e30


def partner_2(block, axis, apart):
    count = lax.axis_size(axis)
    route = []
    for low in range(count):
        high = low | 1 << apart
        if high != low and high < count:
            route += [(low, high), (high, low)]
    return lax.ppermute(block, axis, route)


def norm_rows(rows, gain):
    widened = rows.astype(jnp.float32)
    inverse_rms = lax.rsqrt(jnp.mean(widened * widened, axis=-1, keepdims=True) + norm_epsilon)
    return (widened * inverse_rms * gain).astype(jnp.bfloat16)


def rotate_pairs(values, positions, first_pair):
    width = values.shape[-1]
    pair_count = width // 2
    exponent = 2.0 * (first_pair + jnp.arange(pair_count, dtype=jnp.int32)).astype(jnp.float32) / HD
    frequency = rope_base ** (-exponent)
    angles = positions.astype(jnp.float32)[:, None] * frequency[None, :]
    even_lane = jnp.arange(width, dtype=jnp.int32) % 2 == 0
    cosine = jnp.repeat(jnp.cos(angles), 2, axis=-1)[:, None, :]
    signed_sine = (jnp.repeat(jnp.sin(angles), 2, axis=-1) * jnp.where(even_lane, -1.0, 1.0))[:, None, :]
    swapped = jnp.where(even_lane, jnp.roll(values, -1, axis=-1), jnp.roll(values, 1, axis=-1))
    return values * cosine + swapped * signed_sine


def attend_block(query_block, query_segments, query_index, keys_full, values_full, segment_ids):
    scores = jnp.einsum(
        "qhd,kd->hqk", query_block, keys_full, preferred_element_type=jnp.float32
    ) * HD ** (-0.5)
    key_index = jnp.arange(keys_full.shape[0], dtype=jnp.int32)
    allowed = (query_segments[:, None] == segment_ids[None, :]) & (
        key_index[None, :] <= query_index[:, None]
    )
    scores = jnp.where(allowed[None], scores, masked_score)
    row_top = jnp.max(scores, axis=-1, keepdims=True)
    weights = jnp.exp(scores - row_top)
    probabilities = (weights / jnp.sum(weights, axis=-1, keepdims=True)).astype(jnp.bfloat16)
    mixed_rows = jnp.einsum(
        "hqk,kd->qhd", probabilities, values_full, preferred_element_type=jnp.float32
    )
    return mixed_rows.astype(jnp.bfloat16).reshape(query_block.shape[0], -1)


def shards(
    text_embed,
    bridge,
    crystal_slot,
    segments,
    attn_gain,
    w_query,
    w_key,
    w_value,
    w_out,
    mlp_gain,
    w_gate,
    w_up,
    w_down,
):
    seq_len = text_embed.shape[1]
    part_width = text_embed.shape[2]
    doc_count = seq_len // DOC_LEN
    bridge_len = bridge.shape[1]
    tok_rows = seq_len // lax.axis_size("ts")
    group_index = lax.axis_index("dp")
    ts_index = lax.axis_index("ts")
    segment_ids = segments[0]
    doc_numbers = jnp.arange(doc_count, dtype=jnp.int32)
    starts = jnp.sum((segment_ids[None, :] < doc_numbers[:, None]).astype(jnp.int32), axis=1)
    doc_match = segment_ids[:, None] == doc_numbers[None, :]
    positions = jnp.arange(seq_len, dtype=jnp.int32) - jnp.sum(
        jnp.where(doc_match, starts[None, :], 0), axis=1
    )
    flat_bridge = bridge.reshape(bridge.shape[0], bridge_len * part_width)
    slot_high = (crystal_slot // 128).astype(jnp.bfloat16)
    slot_low = (crystal_slot % 128).astype(jnp.bfloat16)
    slot_cols = jnp.zeros((bridge.shape[0], 128), jnp.bfloat16)
    slot_cols = slot_cols.at[:, 0].set(slot_high).at[:, 1].set(slot_low)
    payload = jnp.concatenate([flat_bridge, slot_cols], axis=1)
    crystal_count = bridge.shape[0]
    destination = crystal_slot // seq_len
    crystal_numbers = jnp.arange(crystal_count, dtype=jnp.int32)
    same_destination = destination[:, None] == destination[None, :]
    rank = jnp.sum(
        (same_destination & (crystal_numbers[None, :] < crystal_numbers[:, None])).astype(jnp.int32),
        axis=1,
    )
    per_destination = crystal_count // lax.axis_size("dp")
    send_row = destination * per_destination + rank
    sending = crystal_numbers[:, None] == send_row[None, :]
    outgoing = jnp.dot(
        sending.astype(jnp.bfloat16), payload, preferred_element_type=jnp.float32
    ).astype(jnp.bfloat16)
    arrived_all = lax.all_to_all(outgoing, "dp", 0, 0, tiled=True)
    arrived = arrived_all[:, : bridge_len * part_width]
    arrived_slots = (
        arrived_all[:, -128].astype(jnp.int32) * 128 + arrived_all[:, -127].astype(jnp.int32)
    )
    wanted = group_index * seq_len + starts
    picking = wanted[:, None] == arrived_slots[None, :]
    by_doc = jnp.dot(
        picking.astype(jnp.bfloat16), arrived, preferred_element_type=jnp.float32
    ).astype(jnp.bfloat16)
    by_doc = by_doc.reshape(doc_count * bridge_len, part_width)
    in_bridge = positions < bridge_len
    row_pick = (segment_ids * bridge_len + positions)[:, None] == jnp.arange(
        doc_count * bridge_len, dtype=jnp.int32
    )[None, :]
    row_pick = row_pick & in_bridge[:, None]
    filled = jnp.dot(
        row_pick.astype(jnp.bfloat16), by_doc, preferred_element_type=jnp.float32
    ).astype(jnp.bfloat16)
    own_part = jnp.where(in_bridge[:, None], filled, text_embed[0])
    ts_count = lax.axis_size("ts")
    stacked = lax.all_gather(own_part, "ts", axis=0, tiled=False)
    positions = lax.optimization_barrier((own_part, positions))[1]
    packed = lax.optimization_barrier(
        stacked.transpose(1, 0, 2).reshape(seq_len, ts_count * part_width)
    )
    widened = stacked.astype(jnp.float32)
    square_sum = jnp.sum(jnp.sum(widened * widened, axis=2), axis=0)
    inverse_rms = lax.rsqrt(square_sum / (ts_count * part_width) + norm_epsilon)
    normed = (
        widened * inverse_rms[None, :, None] * attn_gain.reshape(ts_count, 1, part_width)
    ).astype(jnp.bfloat16)

    def project(weight):
        return jnp.einsum(
            "srk,skn->rn",
            normed,
            weight.reshape(ts_count, part_width, weight.shape[1]),
            preferred_element_type=jnp.float32,
        )

    heads_here = w_query.shape[1] // HD
    queries = project(w_query).reshape(seq_len, heads_here, HD)
    queries = rotate_pairs(queries, positions, 0).astype(jnp.bfloat16)
    kv_cols = w_key.shape[1]
    upper_half = ts_index % 2 == 1
    key_half = project(w_key).reshape(
        seq_len, 1, kv_cols
    )
    key_half = rotate_pairs(key_half, positions, ts_index % 2 * (kv_cols // 2))
    key_half = key_half.astype(jnp.bfloat16).reshape(seq_len, kv_cols)
    value_half = project(w_value).astype(jnp.bfloat16)
    own_pair = jnp.concatenate([key_half, value_half], axis=1)
    partner = partner_2(own_pair, "ts", 0)
    lower_half = jnp.where(upper_half, partner, own_pair)
    higher = jnp.where(upper_half, own_pair, partner)
    keys_full = jnp.concatenate([lower_half[:, :kv_cols], higher[:, :kv_cols]], axis=1)
    values_full = jnp.concatenate([lower_half[:, kv_cols:], higher[:, kv_cols:]], axis=1)
    block_rows = min(512, seq_len)
    outputs = []
    for block_index in range(seq_len // block_rows):
        first_row = block_index * block_rows
        end_row = first_row + block_rows
        query_index = jnp.arange(first_row, end_row, dtype=jnp.int32)
        outputs.append(
            attend_block(
                queries[first_row:end_row],
                segment_ids[first_row:end_row],
                query_index,
                keys_full[:end_row],
                values_full[:end_row],
                segment_ids[:end_row],
            )
        )
    attended = jnp.concatenate(outputs, axis=0)
    mine_offset = ts_index * tok_rows
    partial_rows = jnp.dot(attended, w_out, preferred_element_type=jnp.float32)
    attn_sum = lax.psum(partial_rows.astype(jnp.bfloat16), "ts").astype(jnp.float32)
    after_all = (packed.astype(jnp.float32) + attn_sum).astype(jnp.bfloat16)
    after_mine = lax.dynamic_slice_in_dim(after_all, mine_offset, tok_rows, 0)
    normed_mlp = norm_rows(after_all, mlp_gain)
    gate_proj = jnp.dot(normed_mlp, w_gate, preferred_element_type=jnp.float32)
    up_proj = jnp.dot(normed_mlp, w_up, preferred_element_type=jnp.float32)
    hidden = (jax.nn.silu(gate_proj) * up_proj).astype(jnp.bfloat16)
    mlp_mine = lax.psum_scatter(
        jnp.dot(hidden, w_down, preferred_element_type=jnp.float32).astype(jnp.bfloat16),
        "ts",
        scatter_dimension=0,
        tiled=True,
    ).astype(jnp.float32)
    layer_rows = (after_mine.astype(jnp.float32) + mlp_mine).astype(jnp.bfloat16)
    return layer_rows.reshape(1, tok_rows, layer_rows.shape[1])


def solution(mesh):
    return jax.shard_map(
        shards,
        mesh=mesh,
        in_specs=(
            P("dp", None, "ts"),
            P("dp", None, "ts"),
            P("dp"),
            P("dp", None),
            P(),
            P(None, "ts"),
            P(None, "ts"),
            P(None, "ts"),
            P("ts", None),
            P(),
            P(None, "ts"),
            P(None, "ts"),
            P("ts", None),
        ),
        out_specs=P("dp", "ts", None),
        check_vma=False,
    )
```

```python
import jax
import jax.numpy as jnp
from jax import lax
from jax.sharding import PartitionSpec as P

HD = 128
DOC_LEN = 64


norm_epsilon = 1e-05
rope_base = 500000.0
masked_score = -1e30


def partner_2(block, axis, apart):
    count = lax.axis_size(axis)
    route = []
    for low in range(count):
        high = low | 1 << apart
        if high != low and high < count:
            route += [(low, high), (high, low)]
    return lax.ppermute(block, axis, route)


def norm_rows(rows, gain):
    widened = rows.astype(jnp.float32)
    inverse_rms = lax.rsqrt(jnp.mean(widened * widened, axis=-1, keepdims=True) + norm_epsilon)
    return (widened * inverse_rms * gain).astype(jnp.bfloat16)


def rotate_pairs(values, positions, first_pair):
    width = values.shape[-1]
    pair_count = width // 2
    exponent = 2.0 * (first_pair + jnp.arange(pair_count, dtype=jnp.int32)).astype(jnp.float32) / HD
    frequency = rope_base ** (-exponent)
    angles = positions.astype(jnp.float32)[:, None] * frequency[None, :]
    even_lane = jnp.arange(width, dtype=jnp.int32) % 2 == 0
    cosine = jnp.repeat(jnp.cos(angles), 2, axis=-1)[:, None, :]
    signed_sine = (jnp.repeat(jnp.sin(angles), 2, axis=-1) * jnp.where(even_lane, -1.0, 1.0))[:, None, :]
    swapped = jnp.where(even_lane, jnp.roll(values, -1, axis=-1), jnp.roll(values, 1, axis=-1))
    return values * cosine + swapped * signed_sine


def attend_block(query_block, query_segments, query_index, keys_full, values_full, segment_ids):
    scores = jnp.einsum(
        "qhd,kd->hqk", query_block, keys_full, preferred_element_type=jnp.float32
    ) * HD ** (-0.5)
    key_index = jnp.arange(keys_full.shape[0], dtype=jnp.int32)
    allowed = (query_segments[:, None] == segment_ids[None, :]) & (
        key_index[None, :] <= query_index[:, None]
    )
    scores = jnp.where(allowed[None], scores, masked_score)
    row_top = jnp.max(scores, axis=-1, keepdims=True)
    weights = jnp.exp(scores - row_top)
    probabilities = (weights / jnp.sum(weights, axis=-1, keepdims=True)).astype(jnp.bfloat16)
    mixed_rows = jnp.einsum(
        "hqk,kd->qhd", probabilities, values_full, preferred_element_type=jnp.float32
    )
    return mixed_rows.astype(jnp.bfloat16).reshape(query_block.shape[0], -1)


def shards(
    text_embed,
    bridge,
    crystal_slot,
    segments,
    attn_gain,
    w_query,
    w_key,
    w_value,
    w_out,
    mlp_gain,
    w_gate,
    w_up,
    w_down,
):
    seq_len = text_embed.shape[1]
    part_width = text_embed.shape[2]
    doc_count = seq_len // DOC_LEN
    bridge_len = bridge.shape[1]
    tok_rows = seq_len // lax.axis_size("ts")
    group_index = lax.axis_index("dp")
    ts_index = lax.axis_index("ts")
    segment_ids = segments[0]
    doc_numbers = jnp.arange(doc_count, dtype=jnp.int32)
    starts = jnp.sum((segment_ids[None, :] < doc_numbers[:, None]).astype(jnp.int32), axis=1)
    doc_match = segment_ids[:, None] == doc_numbers[None, :]
    positions = jnp.arange(seq_len, dtype=jnp.int32) - jnp.sum(
        jnp.where(doc_match, starts[None, :], 0), axis=1
    )
    flat_bridge = bridge.reshape(bridge.shape[0], bridge_len * part_width)
    slot_high = (crystal_slot // 128).astype(jnp.bfloat16)
    slot_low = (crystal_slot % 128).astype(jnp.bfloat16)
    slot_cols = jnp.zeros((bridge.shape[0], 128), jnp.bfloat16)
    slot_cols = slot_cols.at[:, 0].set(slot_high).at[:, 1].set(slot_low)
    payload = jnp.concatenate([flat_bridge, slot_cols], axis=1)
    crystal_count = bridge.shape[0]
    destination = crystal_slot // seq_len
    crystal_numbers = jnp.arange(crystal_count, dtype=jnp.int32)
    same_destination = destination[:, None] == destination[None, :]
    rank = jnp.sum(
        (same_destination & (crystal_numbers[None, :] < crystal_numbers[:, None])).astype(jnp.int32),
        axis=1,
    )
    per_destination = crystal_count // lax.axis_size("dp")
    send_row = destination * per_destination + rank
    sending = crystal_numbers[:, None] == send_row[None, :]
    outgoing = jnp.dot(
        sending.astype(jnp.bfloat16), payload, preferred_element_type=jnp.float32
    ).astype(jnp.bfloat16)
    arrived_all = lax.all_to_all(outgoing, "dp", 0, 0, tiled=True)
    arrived = arrived_all[:, : bridge_len * part_width]
    arrived_slots = (
        arrived_all[:, -128].astype(jnp.int32) * 128 + arrived_all[:, -127].astype(jnp.int32)
    )
    wanted = group_index * seq_len + starts
    picking = wanted[:, None] == arrived_slots[None, :]
    by_doc = jnp.dot(
        picking.astype(jnp.bfloat16), arrived, preferred_element_type=jnp.float32
    ).astype(jnp.bfloat16)
    by_doc = by_doc.reshape(doc_count * bridge_len, part_width)
    in_bridge = positions < bridge_len
    row_pick = (segment_ids * bridge_len + positions)[:, None] == jnp.arange(
        doc_count * bridge_len, dtype=jnp.int32
    )[None, :]
    row_pick = row_pick & in_bridge[:, None]
    filled = jnp.dot(
        row_pick.astype(jnp.bfloat16), by_doc, preferred_element_type=jnp.float32
    ).astype(jnp.bfloat16)
    own_part = jnp.where(in_bridge[:, None], filled, text_embed[0])
    ts_count = lax.axis_size("ts")
    stacked = lax.all_gather(own_part, "ts", axis=0, tiled=False)
    positions = lax.optimization_barrier((own_part, positions))[1]
    packed = lax.optimization_barrier(
        stacked.transpose(1, 0, 2).reshape(seq_len, ts_count * part_width)
    )
    widened = stacked.astype(jnp.float32)
    square_sum = jnp.sum(jnp.sum(widened * widened, axis=2), axis=0)
    inverse_rms = lax.rsqrt(square_sum / (ts_count * part_width) + norm_epsilon)
    normed = (
        widened * inverse_rms[None, :, None] * attn_gain.reshape(ts_count, 1, part_width)
    ).astype(jnp.bfloat16)

    def project(weight):
        return jnp.einsum(
            "srk,skn->rn",
            normed,
            weight.reshape(ts_count, part_width, weight.shape[1]),
            preferred_element_type=jnp.float32,
        )

    kv_cols = w_key.shape[1]
    upper_half = ts_index % 2 == 1
    key_half = project(w_key).reshape(
        seq_len, 1, kv_cols
    )
    key_half = rotate_pairs(key_half, positions, ts_index % 2 * (kv_cols // 2))
    key_half = key_half.astype(jnp.bfloat16).reshape(seq_len, kv_cols)
    value_half = project(w_value).astype(jnp.bfloat16)
    own_pair = jnp.concatenate([key_half, value_half], axis=1)
    partner = partner_2(own_pair, "ts", 0)
    query_weight = lax.optimization_barrier((own_pair, w_query))[1]
    heads_here = w_query.shape[1] // HD
    queries = project(query_weight).reshape(seq_len, heads_here, HD)
    queries = rotate_pairs(queries, positions, 0).astype(jnp.bfloat16)
    lower_half = jnp.where(upper_half, partner, own_pair)
    higher = jnp.where(upper_half, own_pair, partner)
    keys_full = jnp.concatenate([lower_half[:, :kv_cols], higher[:, :kv_cols]], axis=1)
    values_full = jnp.concatenate([lower_half[:, kv_cols:], higher[:, kv_cols:]], axis=1)
    block_rows = min(512, seq_len)
    outputs = []
    for block_index in range(seq_len // block_rows):
        first_row = block_index * block_rows
        end_row = first_row + block_rows
        query_index = jnp.arange(first_row, end_row, dtype=jnp.int32)
        outputs.append(
            attend_block(
                queries[first_row:end_row],
                segment_ids[first_row:end_row],
                query_index,
                keys_full[:end_row],
                values_full[:end_row],
                segment_ids[:end_row],
            )
        )
    attended = jnp.concatenate(outputs, axis=0)
    mine_offset = ts_index * tok_rows
    partial_rows = jnp.dot(attended, w_out, preferred_element_type=jnp.float32)
    attn_sum = lax.psum(partial_rows.astype(jnp.bfloat16), "ts").astype(jnp.float32)
    after_all = (packed.astype(jnp.float32) + attn_sum).astype(jnp.bfloat16)
    after_mine = lax.dynamic_slice_in_dim(after_all, mine_offset, tok_rows, 0)
    normed_mlp = norm_rows(after_all, mlp_gain)
    gate_proj = jnp.dot(normed_mlp, w_gate, preferred_element_type=jnp.float32)
    up_proj = jnp.dot(normed_mlp, w_up, preferred_element_type=jnp.float32)
    hidden = (jax.nn.silu(gate_proj) * up_proj).astype(jnp.bfloat16)
    mlp_mine = lax.psum_scatter(
        jnp.dot(hidden, w_down, preferred_element_type=jnp.float32).astype(jnp.bfloat16),
        "ts",
        scatter_dimension=0,
        tiled=True,
    ).astype(jnp.float32)
    layer_rows = (after_mine.astype(jnp.float32) + mlp_mine).astype(jnp.bfloat16)
    return layer_rows.reshape(1, tok_rows, layer_rows.shape[1])


def solution(mesh):
    return jax.shard_map(
        shards,
        mesh=mesh,
        in_specs=(
            P("dp", None, "ts"),
            P("dp", None, "ts"),
            P("dp"),
            P("dp", None),
            P(),
            P(None, "ts"),
            P(None, "ts"),
            P(None, "ts"),
            P("ts", None),
            P(),
            P(None, "ts"),
            P(None, "ts"),
            P("ts", None),
        ),
        out_specs=P("dp", "ts", None),
        check_vma=False,
    )
```

```python
import jax
import jax.numpy as jnp
from jax import lax
from jax.sharding import PartitionSpec as P

HD = 128
DOC_LEN = 64


norm_epsilon = 1e-05
rope_base = 500000.0
masked_score = -1e30


def partner_2(block, axis, apart):
    count = lax.axis_size(axis)
    route = []
    for low in range(count):
        high = low | 1 << apart
        if high != low and high < count:
            route += [(low, high), (high, low)]
    return lax.ppermute(block, axis, route)


def norm_rows(rows, gain):
    widened = rows.astype(jnp.float32)
    inverse_rms = lax.rsqrt(jnp.mean(widened * widened, axis=-1, keepdims=True) + norm_epsilon)
    return (widened * inverse_rms * gain).astype(jnp.bfloat16)


def rotate_pairs(values, positions, first_pair):
    width = values.shape[-1]
    pair_count = width // 2
    exponent = 2.0 * (first_pair + jnp.arange(pair_count, dtype=jnp.int32)).astype(jnp.float32) / HD
    frequency = rope_base ** (-exponent)
    angles = positions.astype(jnp.float32)[:, None] * frequency[None, :]
    even_lane = jnp.arange(width, dtype=jnp.int32) % 2 == 0
    cosine = jnp.repeat(jnp.cos(angles), 2, axis=-1)[:, None, :]
    signed_sine = (jnp.repeat(jnp.sin(angles), 2, axis=-1) * jnp.where(even_lane, -1.0, 1.0))[:, None, :]
    swapped = jnp.where(even_lane, jnp.roll(values, -1, axis=-1), jnp.roll(values, 1, axis=-1))
    return values * cosine + swapped * signed_sine


def attend_block(query_block, query_segments, query_index, keys_full, values_full, segment_ids):
    scores = jnp.einsum(
        "qhd,kd->hqk", query_block, keys_full, preferred_element_type=jnp.float32
    ) * HD ** (-0.5)
    key_index = jnp.arange(keys_full.shape[0], dtype=jnp.int32)
    allowed = (query_segments[:, None] == segment_ids[None, :]) & (
        key_index[None, :] <= query_index[:, None]
    )
    scores = jnp.where(allowed[None], scores, masked_score)
    row_top = jnp.max(scores, axis=-1, keepdims=True)
    weights = jnp.exp(scores - row_top)
    probabilities = (weights / jnp.sum(weights, axis=-1, keepdims=True)).astype(jnp.bfloat16)
    mixed_rows = jnp.einsum(
        "hqk,kd->qhd", probabilities, values_full, preferred_element_type=jnp.float32
    )
    return mixed_rows.astype(jnp.bfloat16).reshape(query_block.shape[0], -1)


def shards(
    text_embed,
    bridge,
    crystal_slot,
    segments,
    attn_gain,
    w_query,
    w_key,
    w_value,
    w_out,
    mlp_gain,
    w_gate,
    w_up,
    w_down,
):
    seq_len = text_embed.shape[1]
    part_width = text_embed.shape[2]
    doc_count = seq_len // DOC_LEN
    bridge_len = bridge.shape[1]
    tok_rows = seq_len // lax.axis_size("ts")
    group_index = lax.axis_index("dp")
    ts_index = lax.axis_index("ts")
    segment_ids = segments[0]
    doc_numbers = jnp.arange(doc_count, dtype=jnp.int32)
    starts = jnp.sum((segment_ids[None, :] < doc_numbers[:, None]).astype(jnp.int32), axis=1)
    doc_match = segment_ids[:, None] == doc_numbers[None, :]
    positions = jnp.arange(seq_len, dtype=jnp.int32) - jnp.sum(
        jnp.where(doc_match, starts[None, :], 0), axis=1
    )
    flat_bridge = bridge.reshape(bridge.shape[0], bridge_len * part_width)
    slot_high = (crystal_slot // 128).astype(jnp.bfloat16)
    slot_low = (crystal_slot % 128).astype(jnp.bfloat16)
    slot_cols = jnp.zeros((bridge.shape[0], 128), jnp.bfloat16)
    slot_cols = slot_cols.at[:, 0].set(slot_high).at[:, 1].set(slot_low)
    payload = jnp.concatenate([flat_bridge, slot_cols], axis=1)
    crystal_count = bridge.shape[0]
    destination = crystal_slot // seq_len
    crystal_numbers = jnp.arange(crystal_count, dtype=jnp.int32)
    same_destination = destination[:, None] == destination[None, :]
    rank = jnp.sum(
        (same_destination & (crystal_numbers[None, :] < crystal_numbers[:, None])).astype(jnp.int32),
        axis=1,
    )
    per_destination = crystal_count // lax.axis_size("dp")
    send_row = destination * per_destination + rank
    sending = crystal_numbers[:, None] == send_row[None, :]
    outgoing = jnp.dot(
        sending.astype(jnp.bfloat16), payload, preferred_element_type=jnp.float32
    ).astype(jnp.bfloat16)
    arrived_all = lax.all_to_all(outgoing, "dp", 0, 0, tiled=True)
    arrived = arrived_all[:, : bridge_len * part_width]
    arrived_slots = (
        arrived_all[:, -128].astype(jnp.int32) * 128 + arrived_all[:, -127].astype(jnp.int32)
    )
    wanted = group_index * seq_len + starts
    picking = wanted[:, None] == arrived_slots[None, :]
    by_doc = jnp.dot(
        picking.astype(jnp.bfloat16), arrived, preferred_element_type=jnp.float32
    ).astype(jnp.bfloat16)
    by_doc = by_doc.reshape(doc_count * bridge_len, part_width)
    in_bridge = positions < bridge_len
    row_pick = (segment_ids * bridge_len + positions)[:, None] == jnp.arange(
        doc_count * bridge_len, dtype=jnp.int32
    )[None, :]
    row_pick = row_pick & in_bridge[:, None]
    filled = jnp.dot(
        row_pick.astype(jnp.bfloat16), by_doc, preferred_element_type=jnp.float32
    ).astype(jnp.bfloat16)
    own_part = jnp.where(in_bridge[:, None], filled, text_embed[0])
    ts_count = lax.axis_size("ts")
    stacked = lax.all_gather(own_part, "ts", axis=0, tiled=False)
    positions = lax.optimization_barrier((own_part, positions))[1]
    packed = lax.optimization_barrier(
        stacked.transpose(1, 0, 2).reshape(seq_len, ts_count * part_width)
    )
    widened = stacked.astype(jnp.float32)
    square_sum = jnp.sum(jnp.sum(widened * widened, axis=2), axis=0)
    inverse_rms = lax.rsqrt(square_sum / (ts_count * part_width) + norm_epsilon)
    normed = (
        widened * inverse_rms[None, :, None] * attn_gain.reshape(ts_count, 1, part_width)
    ).astype(jnp.bfloat16)

    def project(weight, rows=normed):
        return jnp.einsum(
            "srk,skn->rn",
            rows,
            weight.reshape(ts_count, part_width, weight.shape[1]),
            preferred_element_type=jnp.float32,
        )

    kv_cols = w_key.shape[1]
    upper_half = ts_index % 2 == 1
    key_half = project(w_key).reshape(
        seq_len, 1, kv_cols
    )
    key_half = rotate_pairs(key_half, positions, ts_index % 2 * (kv_cols // 2))
    key_half = key_half.astype(jnp.bfloat16).reshape(seq_len, kv_cols)
    value_half = project(w_value).astype(jnp.bfloat16)
    own_pair = jnp.concatenate([key_half, value_half], axis=1)
    partner = partner_2(own_pair, "ts", 0)
    query_rows = lax.optimization_barrier((own_pair, normed))[1]
    heads_here = w_query.shape[1] // HD
    queries = project(w_query, query_rows).reshape(seq_len, heads_here, HD)
    queries = rotate_pairs(queries, positions, 0).astype(jnp.bfloat16)
    lower_half = jnp.where(upper_half, partner, own_pair)
    higher = jnp.where(upper_half, own_pair, partner)
    keys_full = jnp.concatenate([lower_half[:, :kv_cols], higher[:, :kv_cols]], axis=1)
    values_full = jnp.concatenate([lower_half[:, kv_cols:], higher[:, kv_cols:]], axis=1)
    block_rows = min(512, seq_len)
    outputs = []
    for block_index in range(seq_len // block_rows):
        first_row = block_index * block_rows
        end_row = first_row + block_rows
        query_index = jnp.arange(first_row, end_row, dtype=jnp.int32)
        outputs.append(
            attend_block(
                queries[first_row:end_row],
                segment_ids[first_row:end_row],
                query_index,
                keys_full[:end_row],
                values_full[:end_row],
                segment_ids[:end_row],
            )
        )
    attended = jnp.concatenate(outputs, axis=0)
    mine_offset = ts_index * tok_rows
    partial_rows = jnp.dot(attended, w_out, preferred_element_type=jnp.float32)
    attn_sum = lax.psum(partial_rows.astype(jnp.bfloat16), "ts").astype(jnp.float32)
    after_all = (packed.astype(jnp.float32) + attn_sum).astype(jnp.bfloat16)
    after_mine = lax.dynamic_slice_in_dim(after_all, mine_offset, tok_rows, 0)
    normed_mlp = norm_rows(after_all, mlp_gain)
    gate_proj = jnp.dot(normed_mlp, w_gate, preferred_element_type=jnp.float32)
    up_proj = jnp.dot(normed_mlp, w_up, preferred_element_type=jnp.float32)
    hidden = (jax.nn.silu(gate_proj) * up_proj).astype(jnp.bfloat16)
    mlp_mine = lax.psum_scatter(
        jnp.dot(hidden, w_down, preferred_element_type=jnp.float32).astype(jnp.bfloat16),
        "ts",
        scatter_dimension=0,
        tiled=True,
    ).astype(jnp.float32)
    layer_rows = (after_mine.astype(jnp.float32) + mlp_mine).astype(jnp.bfloat16)
    return layer_rows.reshape(1, tok_rows, layer_rows.shape[1])


def solution(mesh):
    return jax.shard_map(
        shards,
        mesh=mesh,
        in_specs=(
            P("dp", None, "ts"),
            P("dp", None, "ts"),
            P("dp"),
            P("dp", None),
            P(),
            P(None, "ts"),
            P(None, "ts"),
            P(None, "ts"),
            P("ts", None),
            P(),
            P(None, "ts"),
            P(None, "ts"),
            P("ts", None),
        ),
        out_specs=P("dp", "ts", None),
        check_vma=False,
    )
```

```python
import jax
import jax.numpy as jnp
from jax import lax
from jax.sharding import PartitionSpec as P

HD = 128
DOC_LEN = 64


norm_epsilon = 1e-05
rope_base = 500000.0
masked_score = -1e30


def partner_2(block, axis, apart):
    count = lax.axis_size(axis)
    route = []
    for low in range(count):
        high = low | 1 << apart
        if high != low and high < count:
            route += [(low, high), (high, low)]
    return lax.ppermute(block, axis, route)


def norm_rows(rows, gain):
    widened = rows.astype(jnp.float32)
    inverse_rms = lax.rsqrt(jnp.mean(widened * widened, axis=-1, keepdims=True) + norm_epsilon)
    return (widened * inverse_rms * gain).astype(jnp.bfloat16)


def rotate_pairs(values, positions, first_pair):
    width = values.shape[-1]
    pair_count = width // 2
    exponent = 2.0 * (first_pair + jnp.arange(pair_count, dtype=jnp.int32)).astype(jnp.float32) / HD
    frequency = rope_base ** (-exponent)
    angles = positions.astype(jnp.float32)[:, None] * frequency[None, :]
    even_lane = jnp.arange(width, dtype=jnp.int32) % 2 == 0
    cosine = jnp.repeat(jnp.cos(angles), 2, axis=-1)[:, None, :]
    signed_sine = (jnp.repeat(jnp.sin(angles), 2, axis=-1) * jnp.where(even_lane, -1.0, 1.0))[:, None, :]
    swapped = jnp.where(even_lane, jnp.roll(values, -1, axis=-1), jnp.roll(values, 1, axis=-1))
    return values * cosine + swapped * signed_sine


def attend_block(query_block, query_segments, query_index, keys_full, values_full, segment_ids):
    scores = jnp.einsum(
        "qhd,kd->hqk", query_block, keys_full, preferred_element_type=jnp.float32
    ) * HD ** (-0.5)
    key_index = jnp.arange(keys_full.shape[0], dtype=jnp.int32)
    allowed = (query_segments[:, None] == segment_ids[None, :]) & (
        key_index[None, :] <= query_index[:, None]
    )
    scores = jnp.where(allowed[None], scores, masked_score)
    row_top = jnp.max(scores, axis=-1, keepdims=True)
    weights = jnp.exp(scores - row_top)
    probabilities = (weights / jnp.sum(weights, axis=-1, keepdims=True)).astype(jnp.bfloat16)
    mixed_rows = jnp.einsum(
        "hqk,kd->qhd", probabilities, values_full, preferred_element_type=jnp.float32
    )
    return mixed_rows.astype(jnp.bfloat16).reshape(query_block.shape[0], -1)


def shards(
    text_embed,
    bridge,
    crystal_slot,
    segments,
    attn_gain,
    w_query,
    w_key,
    w_value,
    w_out,
    mlp_gain,
    w_gate,
    w_up,
    w_down,
):
    seq_len = text_embed.shape[1]
    part_width = text_embed.shape[2]
    doc_count = seq_len // DOC_LEN
    bridge_len = bridge.shape[1]
    tok_rows = seq_len // lax.axis_size("ts")
    group_index = lax.axis_index("dp")
    ts_index = lax.axis_index("ts")
    segment_ids = segments[0]
    doc_numbers = jnp.arange(doc_count, dtype=jnp.int32)
    starts = jnp.sum((segment_ids[None, :] < doc_numbers[:, None]).astype(jnp.int32), axis=1)
    doc_match = segment_ids[:, None] == doc_numbers[None, :]
    positions = jnp.arange(seq_len, dtype=jnp.int32) - jnp.sum(
        jnp.where(doc_match, starts[None, :], 0), axis=1
    )
    flat_bridge = bridge.reshape(bridge.shape[0], bridge_len * part_width)
    slot_high = (crystal_slot // 128).astype(jnp.bfloat16)
    slot_low = (crystal_slot % 128).astype(jnp.bfloat16)
    slot_cols = jnp.zeros((bridge.shape[0], 128), jnp.bfloat16)
    slot_cols = slot_cols.at[:, 0].set(slot_high).at[:, 1].set(slot_low)
    payload = jnp.concatenate([flat_bridge, slot_cols], axis=1)
    crystal_count = bridge.shape[0]
    destination = crystal_slot // seq_len
    crystal_numbers = jnp.arange(crystal_count, dtype=jnp.int32)
    same_destination = destination[:, None] == destination[None, :]
    rank = jnp.sum(
        (same_destination & (crystal_numbers[None, :] < crystal_numbers[:, None])).astype(jnp.int32),
        axis=1,
    )
    per_destination = crystal_count // lax.axis_size("dp")
    send_row = destination * per_destination + rank
    sending = crystal_numbers[:, None] == send_row[None, :]
    outgoing = jnp.dot(
        sending.astype(jnp.bfloat16), payload, preferred_element_type=jnp.float32
    ).astype(jnp.bfloat16)
    arrived_all = lax.all_to_all(outgoing, "dp", 0, 0, tiled=True)
    arrived = arrived_all[:, : bridge_len * part_width]
    arrived_slots = (
        arrived_all[:, -128].astype(jnp.int32) * 128 + arrived_all[:, -127].astype(jnp.int32)
    )
    wanted = group_index * seq_len + starts
    picking = wanted[:, None] == arrived_slots[None, :]
    by_doc = jnp.dot(
        picking.astype(jnp.bfloat16), arrived, preferred_element_type=jnp.float32
    ).astype(jnp.bfloat16)
    by_doc = by_doc.reshape(doc_count * bridge_len, part_width)
    in_bridge = positions < bridge_len
    row_pick = (segment_ids * bridge_len + positions)[:, None] == jnp.arange(
        doc_count * bridge_len, dtype=jnp.int32
    )[None, :]
    row_pick = row_pick & in_bridge[:, None]
    filled = jnp.dot(
        row_pick.astype(jnp.bfloat16), by_doc, preferred_element_type=jnp.float32
    ).astype(jnp.bfloat16)
    own_part = jnp.where(in_bridge[:, None], filled, text_embed[0])
    ts_count = lax.axis_size("ts")
    stacked = lax.all_gather(own_part, "ts", axis=0, tiled=False)
    positions = lax.optimization_barrier((own_part, positions))[1]
    packed = lax.optimization_barrier(
        stacked.transpose(1, 0, 2).reshape(seq_len, ts_count * part_width)
    )
    widened = stacked.astype(jnp.float32)
    square_sum = jnp.sum(jnp.sum(widened * widened, axis=2), axis=0)
    inverse_rms = lax.rsqrt(square_sum / (ts_count * part_width) + norm_epsilon)
    normed = (
        widened * inverse_rms[None, :, None] * attn_gain.reshape(ts_count, 1, part_width)
    ).astype(jnp.bfloat16)

    def project(weight):
        return jnp.einsum(
            "srk,skn->rn",
            normed,
            weight.reshape(ts_count, part_width, weight.shape[1]),
            preferred_element_type=jnp.float32,
        )

    heads_here = w_query.shape[1] // HD
    queries = project(w_query).reshape(seq_len, heads_here, HD)
    kv_cols = w_key.shape[1]
    upper_half = ts_index % 2 == 1
    key_half = project(w_key).reshape(
        seq_len, 1, kv_cols
    )
    key_half = rotate_pairs(key_half, positions, ts_index % 2 * (kv_cols // 2))
    key_half = key_half.astype(jnp.bfloat16).reshape(seq_len, kv_cols)
    value_half = project(w_value).astype(jnp.bfloat16)
    own_pair = jnp.concatenate([key_half, value_half], axis=1)
    partner = partner_2(own_pair, "ts", 0)
    queries = lax.optimization_barrier((own_pair, queries))[1]
    queries = rotate_pairs(queries, positions, 0).astype(jnp.bfloat16)
    lower_half = jnp.where(upper_half, partner, own_pair)
    higher = jnp.where(upper_half, own_pair, partner)
    keys_full = jnp.concatenate([lower_half[:, :kv_cols], higher[:, :kv_cols]], axis=1)
    values_full = jnp.concatenate([lower_half[:, kv_cols:], higher[:, kv_cols:]], axis=1)
    block_rows = min(512, seq_len)
    outputs = []
    for block_index in range(seq_len // block_rows):
        first_row = block_index * block_rows
        end_row = first_row + block_rows
        query_index = jnp.arange(first_row, end_row, dtype=jnp.int32)
        outputs.append(
            attend_block(
                queries[first_row:end_row],
                segment_ids[first_row:end_row],
                query_index,
                keys_full[:end_row],
                values_full[:end_row],
                segment_ids[:end_row],
            )
        )
    attended = jnp.concatenate(outputs, axis=0)
    mine_offset = ts_index * tok_rows
    partial_rows = jnp.dot(attended, w_out, preferred_element_type=jnp.float32)
    attn_sum = lax.psum(partial_rows.astype(jnp.bfloat16), "ts").astype(jnp.float32)
    after_all = (packed.astype(jnp.float32) + attn_sum).astype(jnp.bfloat16)
    after_mine = lax.dynamic_slice_in_dim(after_all, mine_offset, tok_rows, 0)
    normed_mlp = norm_rows(after_all, mlp_gain)
    gate_proj = jnp.dot(normed_mlp, w_gate, preferred_element_type=jnp.float32)
    up_proj = jnp.dot(normed_mlp, w_up, preferred_element_type=jnp.float32)
    hidden = (jax.nn.silu(gate_proj) * up_proj).astype(jnp.bfloat16)
    mlp_mine = lax.psum_scatter(
        jnp.dot(hidden, w_down, preferred_element_type=jnp.float32).astype(jnp.bfloat16),
        "ts",
        scatter_dimension=0,
        tiled=True,
    ).astype(jnp.float32)
    layer_rows = (after_mine.astype(jnp.float32) + mlp_mine).astype(jnp.bfloat16)
    return layer_rows.reshape(1, tok_rows, layer_rows.shape[1])


def solution(mesh):
    return jax.shard_map(
        shards,
        mesh=mesh,
        in_specs=(
            P("dp", None, "ts"),
            P("dp", None, "ts"),
            P("dp"),
            P("dp", None),
            P(),
            P(None, "ts"),
            P(None, "ts"),
            P(None, "ts"),
            P("ts", None),
            P(),
            P(None, "ts"),
            P(None, "ts"),
            P("ts", None),
        ),
        out_specs=P("dp", "ts", None),
        check_vma=False,
    )
```

```python
import jax
import jax.numpy as jnp
from jax import lax
from jax.sharding import PartitionSpec as P

HD = 128
DOC_LEN = 64


norm_epsilon = 1e-05
rope_base = 500000.0
masked_score = -1e30


def partner_2(block, axis, apart):
    count = lax.axis_size(axis)
    route = []
    for low in range(count):
        high = low | 1 << apart
        if high != low and high < count:
            route += [(low, high), (high, low)]
    return lax.ppermute(block, axis, route)


def norm_rows(rows, gain):
    widened = rows.astype(jnp.float32)
    inverse_rms = lax.rsqrt(jnp.mean(widened * widened, axis=-1, keepdims=True) + norm_epsilon)
    return (widened * inverse_rms * gain).astype(jnp.bfloat16)


def rotate_pairs(values, positions, first_pair):
    width = values.shape[-1]
    pair_count = width // 2
    exponent = 2.0 * (first_pair + jnp.arange(pair_count, dtype=jnp.int32)).astype(jnp.float32) / HD
    frequency = rope_base ** (-exponent)
    angles = positions.astype(jnp.float32)[:, None] * frequency[None, :]
    even_lane = jnp.arange(width, dtype=jnp.int32) % 2 == 0
    cosine = jnp.repeat(jnp.cos(angles), 2, axis=-1)[:, None, :]
    signed_sine = (jnp.repeat(jnp.sin(angles), 2, axis=-1) * jnp.where(even_lane, -1.0, 1.0))[:, None, :]
    swapped = jnp.where(even_lane, jnp.roll(values, -1, axis=-1), jnp.roll(values, 1, axis=-1))
    return values * cosine + swapped * signed_sine


def attend_block(query_block, query_segments, query_index, keys_full, values_full, segment_ids):
    scores = jnp.einsum(
        "qhd,kd->hqk", query_block, keys_full, preferred_element_type=jnp.float32
    ) * HD ** (-0.5)
    key_index = jnp.arange(keys_full.shape[0], dtype=jnp.int32)
    allowed = (query_segments[:, None] == segment_ids[None, :]) & (
        key_index[None, :] <= query_index[:, None]
    )
    scores = jnp.where(allowed[None], scores, masked_score)
    row_top = jnp.max(scores, axis=-1, keepdims=True)
    weights = jnp.exp(scores - row_top)
    probabilities = (weights / jnp.sum(weights, axis=-1, keepdims=True)).astype(jnp.bfloat16)
    mixed_rows = jnp.einsum(
        "hqk,kd->qhd", probabilities, values_full, preferred_element_type=jnp.float32
    )
    return mixed_rows.astype(jnp.bfloat16).reshape(query_block.shape[0], -1)


def shards(
    text_embed,
    bridge,
    crystal_slot,
    segments,
    attn_gain,
    w_query,
    w_key,
    w_value,
    w_out,
    mlp_gain,
    w_gate,
    w_up,
    w_down,
):
    seq_len = text_embed.shape[1]
    part_width = text_embed.shape[2]
    doc_count = seq_len // DOC_LEN
    bridge_len = bridge.shape[1]
    tok_rows = seq_len // lax.axis_size("ts")
    group_index = lax.axis_index("dp")
    ts_index = lax.axis_index("ts")
    segment_ids = segments[0]
    doc_numbers = jnp.arange(doc_count, dtype=jnp.int32)
    starts = jnp.sum((segment_ids[None, :] < doc_numbers[:, None]).astype(jnp.int32), axis=1)
    doc_match = segment_ids[:, None] == doc_numbers[None, :]
    positions = jnp.arange(seq_len, dtype=jnp.int32) - jnp.sum(
        jnp.where(doc_match, starts[None, :], 0), axis=1
    )
    flat_bridge = bridge.reshape(bridge.shape[0], bridge_len * part_width)
    slot_high = (crystal_slot // 128).astype(jnp.bfloat16)
    slot_low = (crystal_slot % 128).astype(jnp.bfloat16)
    slot_cols = jnp.zeros((bridge.shape[0], 128), jnp.bfloat16)
    slot_cols = slot_cols.at[:, 0].set(slot_high).at[:, 1].set(slot_low)
    payload = jnp.concatenate([flat_bridge, slot_cols], axis=1)
    crystal_count = bridge.shape[0]
    destination = crystal_slot // seq_len
    crystal_numbers = jnp.arange(crystal_count, dtype=jnp.int32)
    same_destination = destination[:, None] == destination[None, :]
    rank = jnp.sum(
        (same_destination & (crystal_numbers[None, :] < crystal_numbers[:, None])).astype(jnp.int32),
        axis=1,
    )
    per_destination = crystal_count // lax.axis_size("dp")
    send_row = destination * per_destination + rank
    sending = crystal_numbers[:, None] == send_row[None, :]
    outgoing = jnp.dot(
        sending.astype(jnp.bfloat16), payload, preferred_element_type=jnp.float32
    ).astype(jnp.bfloat16)
    dp_count = lax.axis_size("dp")
    pieces = [lax.dynamic_slice_in_dim(outgoing, group_index * per_destination, per_destination, 0)]
    for step in range(1, dp_count):
        block = lax.dynamic_slice_in_dim(
            outgoing, (group_index + step) % dp_count * per_destination, per_destination, 0
        )
        route = [(low, (low + step) % dp_count) for low in range(dp_count)]
        pieces.append(lax.ppermute(block, "dp", route))
    arrived_all = jnp.concatenate(pieces, axis=0)
    arrived = arrived_all[:, : bridge_len * part_width]
    arrived_slots = (
        arrived_all[:, -128].astype(jnp.int32) * 128 + arrived_all[:, -127].astype(jnp.int32)
    )
    wanted = group_index * seq_len + starts
    picking = wanted[:, None] == arrived_slots[None, :]
    by_doc = jnp.dot(
        picking.astype(jnp.bfloat16), arrived, preferred_element_type=jnp.float32
    ).astype(jnp.bfloat16)
    by_doc = by_doc.reshape(doc_count * bridge_len, part_width)
    in_bridge = positions < bridge_len
    row_pick = (segment_ids * bridge_len + positions)[:, None] == jnp.arange(
        doc_count * bridge_len, dtype=jnp.int32
    )[None, :]
    row_pick = row_pick & in_bridge[:, None]
    filled = jnp.dot(
        row_pick.astype(jnp.bfloat16), by_doc, preferred_element_type=jnp.float32
    ).astype(jnp.bfloat16)
    own_part = jnp.where(in_bridge[:, None], filled, text_embed[0])
    ts_count = lax.axis_size("ts")
    stacked = lax.all_gather(own_part, "ts", axis=0, tiled=False)
    positions = lax.optimization_barrier((own_part, positions))[1]
    packed = lax.optimization_barrier(
        stacked.transpose(1, 0, 2).reshape(seq_len, ts_count * part_width)
    )
    widened = stacked.astype(jnp.float32)
    square_sum = jnp.sum(jnp.sum(widened * widened, axis=2), axis=0)
    inverse_rms = lax.rsqrt(square_sum / (ts_count * part_width) + norm_epsilon)
    normed = (
        widened * inverse_rms[None, :, None] * attn_gain.reshape(ts_count, 1, part_width)
    ).astype(jnp.bfloat16)

    def project(weight):
        return jnp.einsum(
            "srk,skn->rn",
            normed,
            weight.reshape(ts_count, part_width, weight.shape[1]),
            preferred_element_type=jnp.float32,
        )

    heads_here = w_query.shape[1] // HD
    queries = project(w_query).reshape(seq_len, heads_here, HD)
    kv_cols = w_key.shape[1]
    upper_half = ts_index % 2 == 1
    key_half = project(w_key).reshape(
        seq_len, 1, kv_cols
    )
    key_half = rotate_pairs(key_half, positions, ts_index % 2 * (kv_cols // 2))
    key_half = key_half.astype(jnp.bfloat16).reshape(seq_len, kv_cols)
    value_half = project(w_value).astype(jnp.bfloat16)
    own_pair = jnp.concatenate([key_half, value_half], axis=1)
    partner = partner_2(own_pair, "ts", 0)
    queries = lax.optimization_barrier((own_pair, queries))[1]
    queries = rotate_pairs(queries, positions, 0).astype(jnp.bfloat16)
    lower_half = jnp.where(upper_half, partner, own_pair)
    higher = jnp.where(upper_half, own_pair, partner)
    keys_full = jnp.concatenate([lower_half[:, :kv_cols], higher[:, :kv_cols]], axis=1)
    values_full = jnp.concatenate([lower_half[:, kv_cols:], higher[:, kv_cols:]], axis=1)
    block_rows = min(512, seq_len)
    outputs = []
    for block_index in range(seq_len // block_rows):
        first_row = block_index * block_rows
        end_row = first_row + block_rows
        query_index = jnp.arange(first_row, end_row, dtype=jnp.int32)
        outputs.append(
            attend_block(
                queries[first_row:end_row],
                segment_ids[first_row:end_row],
                query_index,
                keys_full[:end_row],
                values_full[:end_row],
                segment_ids[:end_row],
            )
        )
    attended = jnp.concatenate(outputs, axis=0)
    mine_offset = ts_index * tok_rows
    partial_rows = jnp.dot(attended, w_out, preferred_element_type=jnp.float32)
    attn_sum = lax.psum(partial_rows.astype(jnp.bfloat16), "ts").astype(jnp.float32)
    after_all = (packed.astype(jnp.float32) + attn_sum).astype(jnp.bfloat16)
    after_mine = lax.dynamic_slice_in_dim(after_all, mine_offset, tok_rows, 0)
    normed_mlp = norm_rows(after_all, mlp_gain)
    gate_proj = jnp.dot(normed_mlp, w_gate, preferred_element_type=jnp.float32)
    up_proj = jnp.dot(normed_mlp, w_up, preferred_element_type=jnp.float32)
    hidden = (jax.nn.silu(gate_proj) * up_proj).astype(jnp.bfloat16)
    mlp_mine = lax.psum_scatter(
        jnp.dot(hidden, w_down, preferred_element_type=jnp.float32).astype(jnp.bfloat16),
        "ts",
        scatter_dimension=0,
        tiled=True,
    ).astype(jnp.float32)
    layer_rows = (after_mine.astype(jnp.float32) + mlp_mine).astype(jnp.bfloat16)
    return layer_rows.reshape(1, tok_rows, layer_rows.shape[1])


def solution(mesh):
    return jax.shard_map(
        shards,
        mesh=mesh,
        in_specs=(
            P("dp", None, "ts"),
            P("dp", None, "ts"),
            P("dp"),
            P("dp", None),
            P(),
            P(None, "ts"),
            P(None, "ts"),
            P(None, "ts"),
            P("ts", None),
            P(),
            P(None, "ts"),
            P(None, "ts"),
            P("ts", None),
        ),
        out_specs=P("dp", "ts", None),
        check_vma=False,
    )
```

```python
import jax
import jax.numpy as jnp
from jax import lax
from jax.sharding import PartitionSpec as P

HD = 128
DOC_LEN = 64


norm_epsilon = 1e-05
rope_base = 500000.0
masked_score = -1e30


def partner_2(block, axis, apart):
    count = lax.axis_size(axis)
    route = []
    for low in range(count):
        high = low | 1 << apart
        if high != low and high < count:
            route += [(low, high), (high, low)]
    return lax.ppermute(block, axis, route)


def norm_rows(rows, gain):
    widened = rows.astype(jnp.float32)
    inverse_rms = lax.rsqrt(jnp.mean(widened * widened, axis=-1, keepdims=True) + norm_epsilon)
    return (widened * inverse_rms * gain).astype(jnp.bfloat16)


def rotate_pairs(values, positions, first_pair):
    width = values.shape[-1]
    pair_count = width // 2
    exponent = 2.0 * (first_pair + jnp.arange(pair_count, dtype=jnp.int32)).astype(jnp.float32) / HD
    frequency = rope_base ** (-exponent)
    angles = positions.astype(jnp.float32)[:, None] * frequency[None, :]
    even_lane = jnp.arange(width, dtype=jnp.int32) % 2 == 0
    cosine = jnp.repeat(jnp.cos(angles), 2, axis=-1)[:, None, :]
    signed_sine = (jnp.repeat(jnp.sin(angles), 2, axis=-1) * jnp.where(even_lane, -1.0, 1.0))[:, None, :]
    swapped = jnp.where(even_lane, jnp.roll(values, -1, axis=-1), jnp.roll(values, 1, axis=-1))
    return values * cosine + swapped * signed_sine


def attend_block(query_block, query_segments, query_index, keys_full, values_full, segment_ids):
    scores = jnp.einsum(
        "qhd,kd->hqk", query_block, keys_full, preferred_element_type=jnp.float32
    ) * HD ** (-0.5)
    key_index = jnp.arange(keys_full.shape[0], dtype=jnp.int32)
    allowed = (query_segments[:, None] == segment_ids[None, :]) & (
        key_index[None, :] <= query_index[:, None]
    )
    scores = jnp.where(allowed[None], scores, masked_score)
    row_top = jnp.max(scores, axis=-1, keepdims=True)
    weights = jnp.exp(scores - row_top)
    probabilities = (weights / jnp.sum(weights, axis=-1, keepdims=True)).astype(jnp.bfloat16)
    mixed_rows = jnp.einsum(
        "hqk,kd->qhd", probabilities, values_full, preferred_element_type=jnp.float32
    )
    return mixed_rows.astype(jnp.bfloat16).reshape(query_block.shape[0], -1)


def shards(
    text_embed,
    bridge,
    crystal_slot,
    segments,
    attn_gain,
    w_query,
    w_key,
    w_value,
    w_out,
    mlp_gain,
    w_gate,
    w_up,
    w_down,
):
    seq_len = text_embed.shape[1]
    part_width = text_embed.shape[2]
    doc_count = seq_len // DOC_LEN
    bridge_len = bridge.shape[1]
    tok_rows = seq_len // lax.axis_size("ts")
    group_index = lax.axis_index("dp")
    ts_index = lax.axis_index("ts")
    segment_ids = segments[0]
    doc_numbers = jnp.arange(doc_count, dtype=jnp.int32)
    starts = jnp.sum((segment_ids[None, :] < doc_numbers[:, None]).astype(jnp.int32), axis=1)
    doc_match = segment_ids[:, None] == doc_numbers[None, :]
    positions = jnp.arange(seq_len, dtype=jnp.int32) - jnp.sum(
        jnp.where(doc_match, starts[None, :], 0), axis=1
    )
    flat_bridge = bridge.reshape(bridge.shape[0], bridge_len * part_width)
    slot_high = (crystal_slot // 128).astype(jnp.bfloat16)
    slot_low = (crystal_slot % 128).astype(jnp.bfloat16)
    slot_cols = jnp.zeros((bridge.shape[0], 128), jnp.bfloat16)
    slot_cols = slot_cols.at[:, 0].set(slot_high).at[:, 1].set(slot_low)
    payload = jnp.concatenate([flat_bridge, slot_cols], axis=1)
    crystal_count = bridge.shape[0]
    destination = crystal_slot // seq_len
    crystal_numbers = jnp.arange(crystal_count, dtype=jnp.int32)
    same_destination = destination[:, None] == destination[None, :]
    rank = jnp.sum(
        (same_destination & (crystal_numbers[None, :] < crystal_numbers[:, None])).astype(jnp.int32),
        axis=1,
    )
    per_destination = crystal_count // lax.axis_size("dp")
    send_row = destination * per_destination + rank
    sending = crystal_numbers[:, None] == send_row[None, :]
    outgoing = jnp.dot(
        sending.astype(jnp.bfloat16), payload, preferred_element_type=jnp.float32
    ).astype(jnp.bfloat16)
    arrived_all = lax.all_to_all(outgoing, "dp", 0, 0, tiled=True)
    arrived = arrived_all[:, : bridge_len * part_width]
    arrived_slots = (
        arrived_all[:, -128].astype(jnp.int32) * 128 + arrived_all[:, -127].astype(jnp.int32)
    )
    wanted = group_index * seq_len + starts
    picking = wanted[:, None] == arrived_slots[None, :]
    by_doc = jnp.dot(
        picking.astype(jnp.bfloat16), arrived, preferred_element_type=jnp.float32
    ).astype(jnp.bfloat16)
    by_doc = by_doc.reshape(doc_count * bridge_len, part_width)
    in_bridge = positions < bridge_len
    row_pick = (segment_ids * bridge_len + positions)[:, None] == jnp.arange(
        doc_count * bridge_len, dtype=jnp.int32
    )[None, :]
    row_pick = row_pick & in_bridge[:, None]
    filled = jnp.dot(
        row_pick.astype(jnp.bfloat16), by_doc, preferred_element_type=jnp.float32
    ).astype(jnp.bfloat16)
    own_part = jnp.where(in_bridge[:, None], filled, text_embed[0])
    ts_count = lax.axis_size("ts")
    stacked = lax.all_gather(own_part, "ts", axis=0, tiled=False)
    positions = lax.optimization_barrier((own_part, positions))[1]
    packed = lax.optimization_barrier(
        stacked.transpose(1, 0, 2).reshape(seq_len, ts_count * part_width)
    )
    widened = stacked.astype(jnp.float32)
    square_sum = jnp.sum(jnp.sum(widened * widened, axis=2), axis=0)
    inverse_rms = lax.rsqrt(square_sum / (ts_count * part_width) + norm_epsilon)
    normed = (
        widened * inverse_rms[None, :, None] * attn_gain.reshape(ts_count, 1, part_width)
    ).astype(jnp.bfloat16)

    def project(weight):
        return jnp.einsum(
            "srk,skn->rn",
            normed,
            weight.reshape(ts_count, part_width, weight.shape[1]),
            preferred_element_type=jnp.float32,
        )

    heads_here = w_query.shape[1] // HD
    queries = project(w_query).reshape(seq_len, heads_here, HD)
    kv_cols = w_key.shape[1]
    upper_half = ts_index % 2 == 1
    key_half = project(w_key).reshape(
        seq_len, 1, kv_cols
    )
    key_half = rotate_pairs(key_half, positions, ts_index % 2 * (kv_cols // 2))
    key_half = key_half.astype(jnp.bfloat16).reshape(seq_len, kv_cols)
    value_half = project(w_value).astype(jnp.bfloat16)
    own_pair = jnp.concatenate([key_half, value_half], axis=1)
    partner = partner_2(own_pair, "ts", 0)
    queries = lax.optimization_barrier((own_pair, queries))[1]
    queries = rotate_pairs(queries, positions, 0).astype(jnp.bfloat16)
    lower_half = jnp.where(upper_half, partner, own_pair)
    higher = jnp.where(upper_half, own_pair, partner)
    keys_full = jnp.concatenate([lower_half[:, :kv_cols], higher[:, :kv_cols]], axis=1)
    values_full = jnp.concatenate([lower_half[:, kv_cols:], higher[:, kv_cols:]], axis=1)
    block_rows = min(512, seq_len)
    outputs = []
    for block_index in range(seq_len // block_rows):
        first_row = block_index * block_rows
        end_row = first_row + block_rows
        query_index = jnp.arange(first_row, end_row, dtype=jnp.int32)
        outputs.append(
            attend_block(
                queries[first_row:end_row],
                segment_ids[first_row:end_row],
                query_index,
                keys_full[:end_row],
                values_full[:end_row],
                segment_ids[:end_row],
            )
        )
    attended = jnp.concatenate(outputs, axis=0)
    mine_offset = ts_index * tok_rows
    partial_rows = jnp.dot(attended, w_out, preferred_element_type=jnp.float32)
    attn_sum = lax.psum(partial_rows.astype(jnp.bfloat16), "ts").astype(jnp.float32)
    after_all = (packed.astype(jnp.float32) + attn_sum).astype(jnp.bfloat16)
    after_mine = (
        lax.dynamic_slice_in_dim(packed, mine_offset, tok_rows, 0).astype(jnp.float32)
        + lax.dynamic_slice_in_dim(attn_sum, mine_offset, tok_rows, 0)
    ).astype(jnp.bfloat16)
    normed_mlp = norm_rows(after_all, mlp_gain)
    gate_proj = jnp.dot(normed_mlp, w_gate, preferred_element_type=jnp.float32)
    up_proj = jnp.dot(normed_mlp, w_up, preferred_element_type=jnp.float32)
    hidden = (jax.nn.silu(gate_proj) * up_proj).astype(jnp.bfloat16)
    mlp_mine = lax.psum_scatter(
        jnp.dot(hidden, w_down, preferred_element_type=jnp.float32).astype(jnp.bfloat16),
        "ts",
        scatter_dimension=0,
        tiled=True,
    ).astype(jnp.float32)
    layer_rows = (after_mine.astype(jnp.float32) + mlp_mine).astype(jnp.bfloat16)
    return layer_rows.reshape(1, tok_rows, layer_rows.shape[1])


def solution(mesh):
    return jax.shard_map(
        shards,
        mesh=mesh,
        in_specs=(
            P("dp", None, "ts"),
            P("dp", None, "ts"),
            P("dp"),
            P("dp", None),
            P(),
            P(None, "ts"),
            P(None, "ts"),
            P(None, "ts"),
            P("ts", None),
            P(),
            P(None, "ts"),
            P(None, "ts"),
            P("ts", None),
        ),
        out_specs=P("dp", "ts", None),
        check_vma=False,
    )
```

```python
import jax
import jax.numpy as jnp
from jax import lax
from jax.sharding import PartitionSpec as P

HD = 128
DOC_LEN = 64


norm_epsilon = 1e-05
rope_base = 500000.0
masked_score = -1e30


def partner_2(block, axis, apart):
    count = lax.axis_size(axis)
    route = []
    for low in range(count):
        high = low | 1 << apart
        if high != low and high < count:
            route += [(low, high), (high, low)]
    return lax.ppermute(block, axis, route)


def norm_rows(rows, gain):
    widened = rows.astype(jnp.float32)
    inverse_rms = lax.rsqrt(jnp.mean(widened * widened, axis=-1, keepdims=True) + norm_epsilon)
    return (widened * inverse_rms * gain).astype(jnp.bfloat16)


def rotate_pairs(values, positions, first_pair):
    width = values.shape[-1]
    pair_count = width // 2
    exponent = 2.0 * (first_pair + jnp.arange(pair_count, dtype=jnp.int32)).astype(jnp.float32) / HD
    frequency = rope_base ** (-exponent)
    angles = positions.astype(jnp.float32)[:, None] * frequency[None, :]
    even_lane = jnp.arange(width, dtype=jnp.int32) % 2 == 0
    cosine = jnp.repeat(jnp.cos(angles), 2, axis=-1)[:, None, :]
    signed_sine = (jnp.repeat(jnp.sin(angles), 2, axis=-1) * jnp.where(even_lane, -1.0, 1.0))[:, None, :]
    swapped = jnp.where(even_lane, jnp.roll(values, -1, axis=-1), jnp.roll(values, 1, axis=-1))
    return values * cosine + swapped * signed_sine


def attend_block(query_block, query_segments, query_index, keys_full, values_full, segment_ids):
    scores = jnp.einsum(
        "qhd,kd->hqk", query_block, keys_full, preferred_element_type=jnp.float32
    ) * HD ** (-0.5)
    key_index = jnp.arange(keys_full.shape[0], dtype=jnp.int32)
    allowed = (query_segments[:, None] == segment_ids[None, :]) & (
        key_index[None, :] <= query_index[:, None]
    )
    scores = jnp.where(allowed[None], scores, masked_score)
    row_top = jnp.max(scores, axis=-1, keepdims=True)
    weights = jnp.exp(scores - row_top)
    probabilities = (weights / jnp.sum(weights, axis=-1, keepdims=True)).astype(jnp.bfloat16)
    mixed_rows = jnp.einsum(
        "hqk,kd->qhd", probabilities, values_full, preferred_element_type=jnp.float32
    )
    return mixed_rows.astype(jnp.bfloat16).reshape(query_block.shape[0], -1)


def shards(
    text_embed,
    bridge,
    crystal_slot,
    segments,
    attn_gain,
    w_query,
    w_key,
    w_value,
    w_out,
    mlp_gain,
    w_gate,
    w_up,
    w_down,
):
    seq_len = text_embed.shape[1]
    part_width = text_embed.shape[2]
    doc_count = seq_len // DOC_LEN
    bridge_len = bridge.shape[1]
    tok_rows = seq_len // lax.axis_size("ts")
    group_index = lax.axis_index("dp")
    ts_index = lax.axis_index("ts")
    segment_ids = segments[0]
    doc_numbers = jnp.arange(doc_count, dtype=jnp.int32)
    starts = jnp.sum((segment_ids[None, :] < doc_numbers[:, None]).astype(jnp.int32), axis=1)
    doc_match = segment_ids[:, None] == doc_numbers[None, :]
    positions = jnp.arange(seq_len, dtype=jnp.int32) - jnp.sum(
        jnp.where(doc_match, starts[None, :], 0), axis=1
    )
    flat_bridge = bridge.reshape(bridge.shape[0], bridge_len * part_width)
    slot_high = (crystal_slot // 128).astype(jnp.bfloat16)
    slot_low = (crystal_slot % 128).astype(jnp.bfloat16)
    slot_cols = jnp.zeros((bridge.shape[0], 128), jnp.bfloat16)
    slot_cols = slot_cols.at[:, 0].set(slot_high).at[:, 1].set(slot_low)
    payload = jnp.concatenate([flat_bridge, slot_cols], axis=1)
    crystal_count = bridge.shape[0]
    destination = crystal_slot // seq_len
    crystal_numbers = jnp.arange(crystal_count, dtype=jnp.int32)
    same_destination = destination[:, None] == destination[None, :]
    rank = jnp.sum(
        (same_destination & (crystal_numbers[None, :] < crystal_numbers[:, None])).astype(jnp.int32),
        axis=1,
    )
    per_destination = crystal_count // lax.axis_size("dp")
    send_row = destination * per_destination + rank
    sending = crystal_numbers[:, None] == send_row[None, :]
    outgoing = jnp.dot(
        sending.astype(jnp.bfloat16), payload, preferred_element_type=jnp.float32
    ).astype(jnp.bfloat16)
    arrived_all = lax.all_to_all(outgoing, "dp", 0, 0, tiled=True)
    arrived = arrived_all[:, : bridge_len * part_width]
    arrived_slots = (
        arrived_all[:, -128].astype(jnp.int32) * 128 + arrived_all[:, -127].astype(jnp.int32)
    )
    wanted = group_index * seq_len + starts
    picking = wanted[:, None] == arrived_slots[None, :]
    by_doc = jnp.dot(
        picking.astype(jnp.bfloat16), arrived, preferred_element_type=jnp.float32
    ).astype(jnp.bfloat16)
    by_doc = by_doc.reshape(doc_count * bridge_len, part_width)
    in_bridge = positions < bridge_len
    row_pick = (segment_ids * bridge_len + positions)[:, None] == jnp.arange(
        doc_count * bridge_len, dtype=jnp.int32
    )[None, :]
    row_pick = row_pick & in_bridge[:, None]
    filled = jnp.dot(
        row_pick.astype(jnp.bfloat16), by_doc, preferred_element_type=jnp.float32
    ).astype(jnp.bfloat16)
    own_part = jnp.where(in_bridge[:, None], filled, text_embed[0])
    ts_count = lax.axis_size("ts")
    stacked = lax.all_gather(own_part, "ts", axis=0, tiled=False)
    positions = lax.optimization_barrier((own_part, positions))[1]
    packed = lax.optimization_barrier(
        stacked.transpose(1, 0, 2).reshape(seq_len, ts_count * part_width)
    )
    widened = stacked.astype(jnp.float32)
    square_sum = jnp.sum(jnp.sum(widened * widened, axis=2), axis=0)
    inverse_rms = lax.rsqrt(square_sum / (ts_count * part_width) + norm_epsilon)
    normed = (
        widened * inverse_rms[None, :, None] * attn_gain.reshape(ts_count, 1, part_width)
    ).astype(jnp.bfloat16)

    def project(weight):
        return jnp.einsum(
            "srk,skn->rn",
            normed,
            weight.reshape(ts_count, part_width, weight.shape[1]),
            preferred_element_type=jnp.float32,
        )

    heads_here = w_query.shape[1] // HD
    queries = project(w_query).reshape(seq_len, heads_here, HD)
    kv_cols = w_key.shape[1]
    upper_half = ts_index % 2 == 1
    key_half = project(w_key).reshape(
        seq_len, 1, kv_cols
    )
    key_half = rotate_pairs(key_half, positions, ts_index % 2 * (kv_cols // 2))
    key_half = key_half.astype(jnp.bfloat16).reshape(seq_len, kv_cols)
    value_half = project(w_value).astype(jnp.bfloat16)
    own_pair = jnp.concatenate([key_half, value_half], axis=1)
    partner = partner_2(own_pair, "ts", 0)
    queries = lax.optimization_barrier((own_pair, queries))[1]
    queries = rotate_pairs(queries, positions, 0).astype(jnp.bfloat16)
    lower_half = jnp.where(upper_half, partner, own_pair)
    higher = jnp.where(upper_half, own_pair, partner)
    keys_full = jnp.concatenate([lower_half[:, :kv_cols], higher[:, :kv_cols]], axis=1)
    values_full = jnp.concatenate([lower_half[:, kv_cols:], higher[:, kv_cols:]], axis=1)
    block_rows = min(512, seq_len)
    outputs = []
    for block_index in range(seq_len // block_rows):
        first_row = block_index * block_rows
        end_row = first_row + block_rows
        query_index = jnp.arange(first_row, end_row, dtype=jnp.int32)
        outputs.append(
            attend_block(
                queries[first_row:end_row],
                segment_ids[first_row:end_row],
                query_index,
                keys_full[:end_row],
                values_full[:end_row],
                segment_ids[:end_row],
            )
        )
    attended = jnp.concatenate(outputs, axis=0)
    mine_offset = ts_index * tok_rows
    partial_rows = jnp.dot(attended, w_out, preferred_element_type=jnp.float32)
    attn_sum = lax.psum(partial_rows.astype(jnp.bfloat16), "ts").astype(jnp.float32)
    after_all = lax.optimization_barrier(
        (packed.astype(jnp.float32) + attn_sum).astype(jnp.bfloat16)
    )
    after_mine = lax.dynamic_slice_in_dim(after_all, mine_offset, tok_rows, 0)
    normed_mlp = norm_rows(after_all, mlp_gain)
    gate_proj = jnp.dot(normed_mlp, w_gate, preferred_element_type=jnp.float32)
    up_proj = jnp.dot(normed_mlp, w_up, preferred_element_type=jnp.float32)
    hidden = (jax.nn.silu(gate_proj) * up_proj).astype(jnp.bfloat16)
    mlp_mine = lax.psum_scatter(
        jnp.dot(hidden, w_down, preferred_element_type=jnp.float32).astype(jnp.bfloat16),
        "ts",
        scatter_dimension=0,
        tiled=True,
    ).astype(jnp.float32)
    layer_rows = (after_mine.astype(jnp.float32) + mlp_mine).astype(jnp.bfloat16)
    return layer_rows.reshape(1, tok_rows, layer_rows.shape[1])


def solution(mesh):
    return jax.shard_map(
        shards,
        mesh=mesh,
        in_specs=(
            P("dp", None, "ts"),
            P("dp", None, "ts"),
            P("dp"),
            P("dp", None),
            P(),
            P(None, "ts"),
            P(None, "ts"),
            P(None, "ts"),
            P("ts", None),
            P(),
            P(None, "ts"),
            P(None, "ts"),
            P("ts", None),
        ),
        out_specs=P("dp", "ts", None),
        check_vma=False,
    )
```

```python
import jax
import jax.numpy as jnp
from jax import lax
from jax.sharding import PartitionSpec as P

HD = 128
DOC_LEN = 64


norm_epsilon = 1e-05
rope_base = 500000.0
masked_score = -1e30


def partner_2(block, axis, apart):
    count = lax.axis_size(axis)
    route = []
    for low in range(count):
        high = low | 1 << apart
        if high != low and high < count:
            route += [(low, high), (high, low)]
    return lax.ppermute(block, axis, route)


def norm_rows(rows, gain):
    widened = rows.astype(jnp.float32)
    inverse_rms = lax.rsqrt(jnp.mean(widened * widened, axis=-1, keepdims=True) + norm_epsilon)
    return (widened * inverse_rms * gain).astype(jnp.bfloat16)


def rotate_pairs(values, positions, first_pair):
    width = values.shape[-1]
    pair_count = width // 2
    exponent = 2.0 * (first_pair + jnp.arange(pair_count, dtype=jnp.int32)).astype(jnp.float32) / HD
    frequency = rope_base ** (-exponent)
    angles = positions.astype(jnp.float32)[:, None] * frequency[None, :]
    even_lane = jnp.arange(width, dtype=jnp.int32) % 2 == 0
    cosine = jnp.repeat(jnp.cos(angles), 2, axis=-1)[:, None, :]
    signed_sine = (jnp.repeat(jnp.sin(angles), 2, axis=-1) * jnp.where(even_lane, -1.0, 1.0))[:, None, :]
    swapped = jnp.where(even_lane, jnp.roll(values, -1, axis=-1), jnp.roll(values, 1, axis=-1))
    return values * cosine + swapped * signed_sine


def attend_block(query_block, query_segments, query_index, keys_full, values_full, segment_ids):
    scores = jnp.einsum(
        "qhd,kd->hqk", query_block, keys_full, preferred_element_type=jnp.float32
    ) * HD ** (-0.5)
    key_index = jnp.arange(keys_full.shape[0], dtype=jnp.int32)
    allowed = (query_segments[:, None] == segment_ids[None, :]) & (
        key_index[None, :] <= query_index[:, None]
    )
    scores = jnp.where(allowed[None], scores, masked_score)
    row_top = jnp.max(scores, axis=-1, keepdims=True)
    weights = jnp.exp(scores - row_top)
    probabilities = (weights / jnp.sum(weights, axis=-1, keepdims=True)).astype(jnp.bfloat16)
    mixed_rows = jnp.einsum(
        "hqk,kd->qhd", probabilities, values_full, preferred_element_type=jnp.float32
    )
    return mixed_rows.astype(jnp.bfloat16).reshape(query_block.shape[0], -1)


def shards(
    text_embed,
    bridge,
    crystal_slot,
    segments,
    attn_gain,
    w_query,
    w_key,
    w_value,
    w_out,
    mlp_gain,
    w_gate,
    w_up,
    w_down,
):
    seq_len = text_embed.shape[1]
    part_width = text_embed.shape[2]
    doc_count = seq_len // DOC_LEN
    bridge_len = bridge.shape[1]
    tok_rows = seq_len // lax.axis_size("ts")
    group_index = lax.axis_index("dp")
    ts_index = lax.axis_index("ts")
    segment_ids = segments[0]
    doc_numbers = jnp.arange(doc_count, dtype=jnp.int32)
    starts = jnp.sum((segment_ids[None, :] < doc_numbers[:, None]).astype(jnp.int32), axis=1)
    doc_match = segment_ids[:, None] == doc_numbers[None, :]
    positions = jnp.arange(seq_len, dtype=jnp.int32) - jnp.sum(
        jnp.where(doc_match, starts[None, :], 0), axis=1
    )
    flat_bridge = bridge.reshape(bridge.shape[0], bridge_len * part_width)
    slot_high = (crystal_slot // 128).astype(jnp.bfloat16)
    slot_low = (crystal_slot % 128).astype(jnp.bfloat16)
    slot_cols = jnp.zeros((bridge.shape[0], 128), jnp.bfloat16)
    slot_cols = slot_cols.at[:, 0].set(slot_high).at[:, 1].set(slot_low)
    payload = jnp.concatenate([flat_bridge, slot_cols], axis=1)
    crystal_count = bridge.shape[0]
    destination = crystal_slot // seq_len
    crystal_numbers = jnp.arange(crystal_count, dtype=jnp.int32)
    same_destination = destination[:, None] == destination[None, :]
    rank = jnp.sum(
        (same_destination & (crystal_numbers[None, :] < crystal_numbers[:, None])).astype(jnp.int32),
        axis=1,
    )
    per_destination = crystal_count // lax.axis_size("dp")
    send_row = destination * per_destination + rank
    sending = crystal_numbers[:, None] == send_row[None, :]
    outgoing = jnp.dot(
        sending.astype(jnp.bfloat16), payload, preferred_element_type=jnp.float32
    ).astype(jnp.bfloat16)
    arrived_all = lax.all_to_all(outgoing, "dp", 0, 0, tiled=True)
    arrived = arrived_all[:, : bridge_len * part_width]
    arrived_slots = (
        arrived_all[:, -128].astype(jnp.int32) * 128 + arrived_all[:, -127].astype(jnp.int32)
    )
    wanted = group_index * seq_len + starts
    picking = wanted[:, None] == arrived_slots[None, :]
    by_doc = jnp.dot(
        picking.astype(jnp.bfloat16), arrived, preferred_element_type=jnp.float32
    ).astype(jnp.bfloat16)
    by_doc = by_doc.reshape(doc_count * bridge_len, part_width)
    in_bridge = positions < bridge_len
    row_pick = (segment_ids * bridge_len + positions)[:, None] == jnp.arange(
        doc_count * bridge_len, dtype=jnp.int32
    )[None, :]
    row_pick = row_pick & in_bridge[:, None]
    filled = jnp.dot(
        row_pick.astype(jnp.bfloat16), by_doc, preferred_element_type=jnp.float32
    ).astype(jnp.bfloat16)
    own_part = jnp.where(in_bridge[:, None], filled, text_embed[0])
    ts_count = lax.axis_size("ts")
    stacked = lax.all_gather(own_part, "ts", axis=0, tiled=False)
    positions = lax.optimization_barrier((own_part, positions))[1]
    packed = lax.optimization_barrier(
        stacked.transpose(1, 0, 2).reshape(seq_len, ts_count * part_width)
    )
    widened = stacked.astype(jnp.float32)
    square_sum = jnp.sum(jnp.sum(widened * widened, axis=2), axis=0)
    inverse_rms = lax.rsqrt(square_sum / (ts_count * part_width) + norm_epsilon)
    normed = (
        widened * inverse_rms[None, :, None] * attn_gain.reshape(ts_count, 1, part_width)
    ).astype(jnp.bfloat16)

    def project(weight):
        return jnp.einsum(
            "srk,skn->rn",
            normed,
            weight.reshape(ts_count, part_width, weight.shape[1]),
            preferred_element_type=jnp.float32,
        )

    heads_here = w_query.shape[1] // HD
    queries = project(w_query).reshape(seq_len, heads_here, HD)
    kv_cols = w_key.shape[1]
    upper_half = ts_index % 2 == 1
    key_half = project(w_key).reshape(
        seq_len, 1, kv_cols
    )
    key_half = rotate_pairs(key_half, positions, ts_index % 2 * (kv_cols // 2))
    key_half = key_half.astype(jnp.bfloat16).reshape(seq_len, kv_cols)
    value_half = project(w_value).astype(jnp.bfloat16)
    own_pair = jnp.concatenate([key_half, value_half], axis=1)
    partner = partner_2(own_pair, "ts", 0)
    queries = lax.optimization_barrier((own_pair, queries))[1]
    queries = rotate_pairs(queries, positions, 0).astype(jnp.bfloat16)
    lower_half = jnp.where(upper_half, partner, own_pair)
    higher = jnp.where(upper_half, own_pair, partner)
    keys_full = jnp.concatenate([lower_half[:, :kv_cols], higher[:, :kv_cols]], axis=1)
    values_full = jnp.concatenate([lower_half[:, kv_cols:], higher[:, kv_cols:]], axis=1)
    block_rows = min(256, seq_len)
    outputs = []
    for block_index in range(seq_len // block_rows):
        first_row = block_index * block_rows
        end_row = first_row + block_rows
        query_index = jnp.arange(first_row, end_row, dtype=jnp.int32)
        outputs.append(
            attend_block(
                queries[first_row:end_row],
                segment_ids[first_row:end_row],
                query_index,
                keys_full[:end_row],
                values_full[:end_row],
                segment_ids[:end_row],
            )
        )
    attended = jnp.concatenate(outputs, axis=0)
    mine_offset = ts_index * tok_rows
    partial_rows = jnp.dot(attended, w_out, preferred_element_type=jnp.float32)
    attn_sum = lax.psum(partial_rows.astype(jnp.bfloat16), "ts").astype(jnp.float32)
    after_all = (packed.astype(jnp.float32) + attn_sum).astype(jnp.bfloat16)
    after_mine = lax.dynamic_slice_in_dim(after_all, mine_offset, tok_rows, 0)
    normed_mlp = norm_rows(after_all, mlp_gain)
    gate_proj = jnp.dot(normed_mlp, w_gate, preferred_element_type=jnp.float32)
    up_proj = jnp.dot(normed_mlp, w_up, preferred_element_type=jnp.float32)
    hidden = (jax.nn.silu(gate_proj) * up_proj).astype(jnp.bfloat16)
    mlp_mine = lax.psum_scatter(
        jnp.dot(hidden, w_down, preferred_element_type=jnp.float32).astype(jnp.bfloat16),
        "ts",
        scatter_dimension=0,
        tiled=True,
    ).astype(jnp.float32)
    layer_rows = (after_mine.astype(jnp.float32) + mlp_mine).astype(jnp.bfloat16)
    return layer_rows.reshape(1, tok_rows, layer_rows.shape[1])


def solution(mesh):
    return jax.shard_map(
        shards,
        mesh=mesh,
        in_specs=(
            P("dp", None, "ts"),
            P("dp", None, "ts"),
            P("dp"),
            P("dp", None),
            P(),
            P(None, "ts"),
            P(None, "ts"),
            P(None, "ts"),
            P("ts", None),
            P(),
            P(None, "ts"),
            P(None, "ts"),
            P("ts", None),
        ),
        out_specs=P("dp", "ts", None),
        check_vma=False,
    )
```
